128 devices in a mesh: seq: 16 (over y, x), tp: 8 (over z, core).
Axes of the slice: x: 4, y: 4, z: 4, core: 2. Of those that a mesh axis runs over, the one named last changes fastest.
Arguments:
- tokens: bfloat16 [24576, 2048], P('seq'), may hold values from -6 to 6
- w_query: bfloat16 [2048, 2048], P(None, 'tp'), may hold values from -0.125 to 0.125
- w_key: bfloat16 [2048, 2048], P(None, 'tp'), may hold values from -0.125 to 0.125
- w_value: bfloat16 [2048, 2048], P(None, 'tp'), may hold values from -0.125 to 0.125
- w_out: bfloat16 [2048, 2048], P('tp'), may hold values from -0.125 to 0.125
- readers: int32 [192, 192], replicated, may hold values from 0 to 1, as said below
- lengths: int32 [192], replicated, may hold values from 1 to 128, as said below
Outputs:
- attended: bfloat16 [24576, 2048], P('seq', 'tp')
The draws below stay inside these ranges and needn't reach their ends.
Inputs may be any that keep to these rules, and one draw needn't show every extreme that they name: The groups form sessions of consecutive groups, the first starting at group 0; readers[c, e] is 1 exactly where e < c and e lies in the same session as c. lengths[c] is 128 on every group but the last of its session; at least one group has 128 live tokens and one has a single one.
All inputs are finite; a program needn't handle non-finite values.
Results may differ from the reference program's by a relative error of at most 0.009.
Values may be sent and summed in bfloat16 or wider, within the bound.
No kernel may reach another device: no remote copies, remote signals or barrier semaphores. Data moves between devices by JAX's collectives and lax.ppermute only.
A program may use at most 128 MiB of HBM per device.

```python
import jax
import jax.numpy as jnp
from jax import lax

HEADS = 16
HS = 128
D = 2048
CH = 128
TOKENS = 24576
GROUPS = 192


def session_layout(key):
    start_key = jax.random.fold_in(key, 101)
    window_key = jax.random.fold_in(key, 103)
    index = jnp.arange(GROUPS, dtype=jnp.int32)
    period = min(24, max(2, GROUPS // 8))
    starts = jax.random.randint(start_key, (GROUPS,), 0, period, dtype=jnp.int32) == 0
    span = GROUPS // 2
    window_at = jax.random.randint(window_key, (), 0, GROUPS - span + 1, dtype=jnp.int32)
    inside = (index > window_at) & (index < window_at + span)
    starts = jnp.where(inside, False, starts)
    starts = jnp.where(index == 0, True, starts)
    session_ids = jnp.cumsum(starts.astype(jnp.int32)) - 1
    next_start = jnp.concatenate([starts[1:], jnp.ones((1,), dtype=bool)])
    return (session_ids.astype(jnp.int32), next_start)


def draw_readers(key, part):
    session_ids, next_start = session_layout(key)
    row_index = jnp.arange(GROUPS, dtype=jnp.int32)[:, None]
    col_index = jnp.arange(GROUPS, dtype=jnp.int32)[None, :]
    same = session_ids[:, None] == session_ids[None, :]
    return jnp.where((row_index > col_index) & same, 1, 0).astype(jnp.int32)


def draw_lengths(key, part):
    session_ids, last_group = session_layout(key)
    tail_key = jax.random.fold_in(key, 107)
    pick_key = jax.random.fold_in(key, 109)
    tails = jax.random.randint(tail_key, (GROUPS,), 1, CH + 1, dtype=jnp.int32)
    ranks = jax.random.permutation(pick_key, GROUPS).astype(jnp.int32)
    chosen = jnp.argmax(jnp.where(last_group, ranks, -1))
    index = jnp.arange(GROUPS, dtype=jnp.int32)
    tails = jnp.where(index == chosen, 1, tails)
    return jnp.where(last_group, tails, CH).astype(jnp.int32)


def shard_levels(rng, extent, shards, low, largest):
    def one(axis_at, blocks):
        draws = jax.random.uniform(jax.random.fold_in(jax.random.fold_in(rng, 6), axis_at), (blocks,), jnp.float32, low / len(shards), largest / len(shards))
        return jnp.repeat(jnp.exp(draws), extent[axis_at] // blocks).reshape((-1,) + (1,) * (len(extent) - axis_at - 1))

    gain = one(*shards[0])
    for cut in shards[1:]:
        gain = gain * one(*cut)
    return gain


def scatter_about(rng, shape, spread, bound, pieces=(), kind=jnp.bfloat16):
    drawn = spread * jax.random.normal(rng, shape, jnp.float32)
    if pieces:
        drawn = drawn * shard_levels(rng, shape, pieces, -0.22, 0.18)
    return jnp.clip(drawn, -bound, bound).astype(kind)


def setup_inputs(seed: int = 0) -> dict:
    keys = jax.random.split(jax.random.key(seed), 8)
    tokens = scatter_about(keys[0], (TOKENS, D), 1.0, 6.0, ((0, 16),))
    w_query = scatter_about(keys[1], (D, D), D ** -0.5, 0.125, ((1, 8),))
    w_key = scatter_about(keys[2], (D, D), D ** -0.5, 0.125, ((1, 8),))
    w_value = scatter_about(keys[3], (D, D), D ** -0.5, 0.125, ((1, 8),))
    w_out = scatter_about(keys[4], (D, D), D ** -0.5, 0.125, ((0, 8),))
    readers = draw_readers(jax.random.fold_in(keys[7], 71), 0)
    lengths = draw_lengths(jax.random.fold_in(keys[7], 71), 0)
    return {"tokens": tokens, "w_query": w_query, "w_key": w_key, "w_value": w_value, "w_out": w_out, "readers": readers, "lengths": lengths}


def reference(tokens, w_query, w_key, w_value, w_out, readers, lengths):
    group_count = tokens.shape[0] // CH
    offsets = jnp.arange(CH, dtype=jnp.int32)
    live_mask = (offsets[None, :] < lengths[:, None]).reshape(-1)[:, None]
    query_rows = jnp.dot(tokens, w_query, preferred_element_type=jnp.float32).astype(jnp.bfloat16)
    key_rows = jnp.where(live_mask, jnp.dot(tokens, w_key, preferred_element_type=jnp.float32), 0.0).astype(jnp.bfloat16)
    value_rows = jnp.where(live_mask, jnp.dot(tokens, w_value, preferred_element_type=jnp.float32), 0.0).astype(jnp.bfloat16)
    query_blocks = query_rows.reshape(group_count, CH, HEADS, HS).astype(jnp.float32)
    key_blocks = key_rows.reshape(group_count, CH, HEADS, HS).astype(jnp.float32)
    value_blocks = value_rows.reshape(group_count, CH, HEADS, HS).astype(jnp.float32)
    states = jnp.einsum('cshd,cshe->chde', key_blocks, value_blocks).astype(jnp.bfloat16)
    prefix = jnp.einsum('cx,xhde->chde', readers.astype(jnp.float32), states.astype(jnp.float32)).astype(jnp.bfloat16)
    carried = jnp.einsum('cthd,chde->cthe', query_blocks, prefix.astype(jnp.float32))
    scores = jnp.einsum('cthd,cshd->chts', query_blocks, key_blocks)
    causal = offsets[:, None] >= offsets[None, :]
    weights = jnp.where(causal[None, None], scores, 0.0).astype(jnp.bfloat16)
    within = jnp.einsum('chts,cshe->cthe', weights.astype(jnp.float32), value_blocks)
    length_float = lengths.astype(jnp.float32)
    keys_read = length_float + jnp.dot(readers.astype(jnp.float32), length_float, precision=lax.Precision.HIGHEST)
    row_scale = lax.rsqrt(HS * keys_read)
    mixed = (carried + within) * row_scale[:, None, None, None]
    mixed = jnp.where(live_mask.reshape(group_count, CH, 1, 1), mixed, 0.0).astype(jnp.bfloat16)
    mixed = mixed.reshape(group_count * CH, HEADS * HS)
    return jnp.dot(mixed, w_out, preferred_element_type=jnp.float32).astype(jnp.bfloat16)
```

```python
import jax
import jax.numpy as jnp
from jax import lax
from jax.sharding import PartitionSpec as P

HS = 128
CH = 128


def local(tokens, w_query, w_key, w_value, w_out, readers, lengths):
    group_local = tokens.shape[0] // CH
    local_width = w_query.shape[1]
    head_dev = local_width // HS
    seq_count = readers.shape[0] // group_local
    first_group = lax.axis_index("seq") * group_local

    tp_count = w_out.shape[1] // local_width
    w_out_cols = lax.all_to_all(
        w_out.reshape(local_width, tp_count, local_width), "tp", 1, 0, tiled=True
    ).reshape(tp_count * local_width, local_width)

    local_lengths = lax.dynamic_slice_in_dim(lengths, first_group, group_local, 0)
    reader_rows = lax.dynamic_slice_in_dim(readers, first_group, group_local, 0)
    offsets = jnp.arange(CH, dtype=jnp.int32)
    live_mask = (offsets[None, :] < local_lengths[:, None]).reshape(-1)[:, None]
    key_rows = jnp.where(
        live_mask, jnp.dot(tokens, w_key, preferred_element_type=jnp.float32), 0.0
    ).astype(jnp.bfloat16)
    value_rows = jnp.where(
        live_mask, jnp.dot(tokens, w_value, preferred_element_type=jnp.float32), 0.0
    ).astype(jnp.bfloat16)
    query_rows = jnp.dot(tokens, w_query, preferred_element_type=jnp.float32).astype(jnp.bfloat16)
    query_blocks = query_rows.reshape(group_local, CH, head_dev, HS)
    key_blocks = key_rows.reshape(group_local, CH, head_dev, HS)
    value_blocks = value_rows.reshape(group_local, CH, head_dev, HS)

    states = jnp.einsum(
        "cshd,cshe->chde", key_blocks, value_blocks, preferred_element_type=jnp.float32
    ).astype(jnp.bfloat16)

    local_readers = lax.dynamic_slice_in_dim(reader_rows, first_group, group_local, 1)
    last_row = local_readers[group_local - 1].at[group_local - 1].set(1)
    states_f32 = states.astype(jnp.float32)
    tail = jnp.einsum(
        "c,chde->hde",
        last_row.astype(jnp.float32),
        states_f32,
        precision=lax.Precision.HIGHEST,
        preferred_element_type=jnp.float32,
    )
    tails = lax.all_gather(tail, "seq", axis=0, tiled=False)
    tail_weights = reader_rows.reshape(group_local, seq_count, group_local)[:, :, group_local - 1]
    carried_in = jnp.einsum(
        "cd,dhij->chij",
        tail_weights.astype(jnp.float32),
        tails,
        precision=lax.Precision.HIGHEST,
        preferred_element_type=jnp.float32,
    )
    own = jnp.einsum(
        "ce,ehij->chij",
        local_readers.astype(jnp.float32),
        states_f32,
        precision=lax.Precision.HIGHEST,
        preferred_element_type=jnp.float32,
    )
    prefix = (carried_in + own).astype(jnp.bfloat16)

    carried = jnp.einsum(
        "cthd,chde->cthe", query_blocks, prefix, preferred_element_type=jnp.float32
    )
    scores = jnp.einsum(
        "cthd,cshd->chts", query_blocks, key_blocks, preferred_element_type=jnp.float32
    )
    causal = offsets[:, None] >= offsets[None, :]
    weights = jnp.where(causal[None, None], scores, 0.0).astype(jnp.bfloat16)
    within = jnp.einsum(
        "chts,cshe->cthe", weights, value_blocks, preferred_element_type=jnp.float32
    )
    length_float = lengths.astype(jnp.float32)
    keys_read = local_lengths.astype(jnp.float32) + jnp.dot(
        reader_rows.astype(jnp.float32), length_float, precision=lax.Precision.HIGHEST
    )
    row_scale = lax.rsqrt(HS * keys_read)
    mixed = (carried + within) * row_scale[:, None, None, None]
    mixed = jnp.where(live_mask.reshape(group_local, CH, 1, 1), mixed, 0.0).astype(jnp.bfloat16)
    mixed = mixed.reshape(group_local * CH, local_width)
    mixed_all = lax.all_gather(mixed, "tp", axis=1, tiled=True)
    return jnp.dot(mixed_all, w_out_cols, preferred_element_type=jnp.float32).astype(jnp.bfloat16)


def solution(mesh):
    return jax.shard_map(
        local,
        mesh=mesh,
        in_specs=(
            P("seq", None),
            P(None, "tp"),
            P(None, "tp"),
            P(None, "tp"),
            P("tp", None),
            P(),
            P(),
        ),
        out_specs=P("seq", "tp"),
        check_vma=False,
    )
```

```python
import jax
import jax.numpy as jnp
from jax import lax
from jax.sharding import PartitionSpec as P

HS = 128
CH = 128


def local(tokens, w_query, w_key, w_value, w_out, readers, lengths):
    group_local = tokens.shape[0] // CH
    local_width = w_query.shape[1]
    head_dev = local_width // HS
    seq_count = readers.shape[0] // group_local
    first_group = lax.axis_index("seq") * group_local

    tp_count = w_out.shape[1] // local_width
    tp_index = lax.axis_index("tp")
    seq_index = lax.axis_index("seq")
    out_blocks = w_out.reshape(local_width, tp_count, local_width)
    w_out_cols = jnp.zeros((tp_count, local_width, local_width), w_out.dtype)
    for shift in range(tp_count):
        piece = lax.dynamic_index_in_dim(out_blocks, (tp_index + shift) % tp_count, 1, False)
        if shift:
            pairs = [(i, (i + shift) % tp_count) for i in range(tp_count)]
            piece = lax.ppermute(piece, "tp", pairs)
        w_out_cols = lax.dynamic_update_index_in_dim(
            w_out_cols, piece, (tp_index - shift) % tp_count, 0
        )
    w_out_cols = w_out_cols.reshape(tp_count * local_width, local_width)

    local_lengths = lax.dynamic_slice_in_dim(lengths, first_group, group_local, 0)
    reader_rows = lax.dynamic_slice_in_dim(readers, first_group, group_local, 0)
    offsets = jnp.arange(CH, dtype=jnp.int32)
    live_mask = (offsets[None, :] < local_lengths[:, None]).reshape(-1)[:, None]
    key_rows = jnp.where(
        live_mask, jnp.dot(tokens, w_key, preferred_element_type=jnp.float32), 0.0
    ).astype(jnp.bfloat16)
    value_rows = jnp.where(
        live_mask, jnp.dot(tokens, w_value, preferred_element_type=jnp.float32), 0.0
    ).astype(jnp.bfloat16)
    query_rows = jnp.dot(tokens, w_query, preferred_element_type=jnp.float32).astype(jnp.bfloat16)
    query_blocks = query_rows.reshape(group_local, CH, head_dev, HS)
    key_blocks = key_rows.reshape(group_local, CH, head_dev, HS)
    value_blocks = value_rows.reshape(group_local, CH, head_dev, HS)

    states = jnp.einsum(
        "cshd,cshe->chde", key_blocks, value_blocks, preferred_element_type=jnp.float32
    ).astype(jnp.bfloat16)

    local_readers = lax.dynamic_slice_in_dim(reader_rows, first_group, group_local, 1)
    last_row = local_readers[group_local - 1].at[group_local - 1].set(1)
    tail = jnp.einsum(
        "c,chde->hde", last_row.astype(jnp.bfloat16), states, preferred_element_type=jnp.float32
    )
    last_group = first_group + group_local - 1
    scan = tail
    shift = 1
    while shift < seq_count:
        source = jnp.maximum(seq_index - shift, 0) * group_local + group_local - 1
        joined = jnp.where(seq_index >= shift, readers[last_group, source], 0).astype(jnp.float32)
        pairs = [(i, i + shift) for i in range(seq_count - shift)]
        scan = scan + joined * lax.ppermute(scan, "seq", pairs)
        shift *= 2
    before = lax.ppermute(scan, "seq", [(i, i + 1) for i in range(seq_count - 1)])
    enters = jnp.where(
        seq_index > 0, lax.dynamic_index_in_dim(reader_rows, first_group - 1, 1, False), 0
    ).astype(jnp.float32)
    carried_in = enters[:, None, None, None] * before[None]
    own = jnp.einsum(
        "ce,ehij->chij",
        local_readers.astype(jnp.bfloat16),
        states,
        preferred_element_type=jnp.float32,
    )
    prefix = (carried_in + own).astype(jnp.bfloat16)

    carried = jnp.einsum(
        "cthd,chde->cthe", query_blocks, prefix, preferred_element_type=jnp.float32
    )
    scores = jnp.einsum(
        "cthd,cshd->chts", query_blocks, key_blocks, preferred_element_type=jnp.float32
    )
    causal = offsets[:, None] >= offsets[None, :]
    weights = jnp.where(causal[None, None], scores, 0.0).astype(jnp.bfloat16)
    within = jnp.einsum(
        "chts,cshe->cthe", weights, value_blocks, preferred_element_type=jnp.float32
    )
    length_float = lengths.astype(jnp.float32)
    keys_read = local_lengths.astype(jnp.float32) + jnp.dot(
        reader_rows.astype(jnp.float32), length_float, precision=lax.Precision.HIGHEST
    )
    row_scale = lax.rsqrt(HS * keys_read)
    mixed = (carried + within) * row_scale[:, None, None, None]
    mixed = jnp.where(live_mask.reshape(group_local, CH, 1, 1), mixed, 0.0).astype(jnp.bfloat16)
    mixed = mixed.reshape(group_local * CH, local_width)
    mixed_all = lax.all_gather(mixed, "tp", axis=1, tiled=True)
    return jnp.dot(mixed_all, w_out_cols, preferred_element_type=jnp.float32).astype(jnp.bfloat16)


def solution(mesh):
    return jax.shard_map(
        local,
        mesh=mesh,
        in_specs=(
            P("seq", None),
            P(None, "tp"),
            P(None, "tp"),
            P(None, "tp"),
            P("tp", None),
            P(),
            P(),
        ),
        out_specs=P("seq", "tp"),
        check_vma=False,
    )
```

```python
import jax
import jax.numpy as jnp
from jax import lax
from jax.sharding import PartitionSpec as P

HS = 128
CH = 128


def local(tokens, w_query, w_key, w_value, w_out, readers, lengths):
    group_local = tokens.shape[0] // CH
    local_width = w_query.shape[1]
    head_dev = local_width // HS
    seq_count = readers.shape[0] // group_local
    first_group = lax.axis_index("seq") * group_local

    tp_count = w_out.shape[1] // local_width
    tp_index = lax.axis_index("tp")
    seq_index = lax.axis_index("seq")
    out_blocks = w_out.reshape(local_width, tp_count, local_width)
    w_out_cols = jnp.zeros((tp_count, local_width, local_width), w_out.dtype)
    for shift in range(tp_count):
        piece = lax.dynamic_index_in_dim(out_blocks, (tp_index + shift) % tp_count, 1, False)
        if shift:
            pairs = [(i, (i + shift) % tp_count) for i in range(tp_count)]
            piece = lax.ppermute(piece, "tp", pairs)
        w_out_cols = lax.dynamic_update_index_in_dim(
            w_out_cols, piece, (tp_index - shift) % tp_count, 0
        )
    w_out_cols = w_out_cols.reshape(tp_count * local_width, local_width)

    local_lengths = lax.dynamic_slice_in_dim(lengths, first_group, group_local, 0)
    reader_rows = lax.dynamic_slice_in_dim(readers, first_group, group_local, 0)
    offsets = jnp.arange(CH, dtype=jnp.int32)
    live_mask = (offsets[None, :] < local_lengths[:, None]).reshape(-1)[:, None]
    key_rows = jnp.where(
        live_mask, jnp.dot(tokens, w_key, preferred_element_type=jnp.float32), 0.0
    ).astype(jnp.bfloat16)
    value_rows = jnp.where(
        live_mask, jnp.dot(tokens, w_value, preferred_element_type=jnp.float32), 0.0
    ).astype(jnp.bfloat16)
    w_query, w_out_cols = lax.optimization_barrier((w_query, w_out_cols))
    query_rows = jnp.dot(tokens, w_query, preferred_element_type=jnp.float32).astype(jnp.bfloat16)
    query_blocks = query_rows.reshape(group_local, CH, head_dev, HS)
    key_blocks = key_rows.reshape(group_local, CH, head_dev, HS)
    value_blocks = value_rows.reshape(group_local, CH, head_dev, HS)

    states = jnp.einsum(
        "cshd,cshe->chde", key_blocks, value_blocks, preferred_element_type=jnp.float32
    ).astype(jnp.bfloat16)

    local_readers = lax.dynamic_slice_in_dim(reader_rows, first_group, group_local, 1)
    last_row = local_readers[group_local - 1].at[group_local - 1].set(1)
    tail = jnp.einsum(
        "c,chde->hde", last_row.astype(jnp.bfloat16), states, preferred_element_type=jnp.float32
    )
    first_reader = first_group
    last_reader = first_group + group_local - 1
    inclusive = tail
    entering = jnp.zeros_like(tail)
    span = 1
    while span < seq_count:
        step_inclusive = inclusive
        for j in range(1, 4):
            shift = j * span
            if shift >= seq_count:
                break
            pairs = [(i, i + shift) for i in range(seq_count - shift)]
            moved = lax.ppermute(inclusive, "seq", pairs)
            source = jnp.maximum(seq_index - shift, 0) * group_local + group_local - 1
            has = seq_index >= shift
            to_last = jnp.where(has, readers[last_reader, source], 0).astype(jnp.float32)
            to_first = jnp.where(has, readers[first_reader, source], 0).astype(jnp.float32)
            step_inclusive = step_inclusive + to_last * moved
            entering = entering + to_first * moved
        inclusive = step_inclusive
        span *= 4
    enters = local_readers[:, 0].at[0].set(1).astype(jnp.float32)
    carried_in = enters[:, None, None, None] * entering[None]
    own = jnp.einsum(
        "ce,ehij->chij",
        local_readers.astype(jnp.bfloat16),
        states,
        preferred_element_type=jnp.float32,
    )
    prefix = (carried_in + own).astype(jnp.bfloat16)

    carried = jnp.einsum(
        "cthd,chde->cthe", query_blocks, prefix, preferred_element_type=jnp.float32
    )
    scores = jnp.einsum(
        "cthd,cshd->chts", query_blocks, key_blocks, preferred_element_type=jnp.float32
    )
    causal = offsets[:, None] >= offsets[None, :]
    weights = jnp.where(causal[None, None], scores, 0.0).astype(jnp.bfloat16)
    within = jnp.einsum(
        "chts,cshe->cthe", weights, value_blocks, preferred_element_type=jnp.float32
    )
    length_float = lengths.astype(jnp.float32)
    keys_read = local_lengths.astype(jnp.float32) + jnp.dot(
        reader_rows.astype(jnp.float32), length_float, precision=lax.Precision.HIGHEST
    )
    row_scale = lax.rsqrt(HS * keys_read)
    mixed = (carried + within) * row_scale[:, None, None, None]
    mixed = jnp.where(live_mask.reshape(group_local, CH, 1, 1), mixed, 0.0).astype(jnp.bfloat16)
    mixed = mixed.reshape(group_local * CH, local_width)
    mixed_all = lax.all_gather(mixed, "tp", axis=1, tiled=True)
    return jnp.dot(mixed_all, w_out_cols, preferred_element_type=jnp.float32).astype(jnp.bfloat16)


def solution(mesh):
    return jax.shard_map(
        local,
        mesh=mesh,
        in_specs=(
            P("seq", None),
            P(None, "tp"),
            P(None, "tp"),
            P(None, "tp"),
            P("tp", None),
            P(),
            P(),
        ),
        out_specs=P("seq", "tp"),
        check_vma=False,
    )
```

```python
import jax
import jax.numpy as jnp
from jax import lax
from jax.sharding import PartitionSpec as P

HS = 128
CH = 128
ROW = 4
PAIR = 2


SEQ = ("sy", "sx")
TP = ("tz", "tc")


def local(tokens, w_query, w_key, w_value, w_out, readers, lengths):
    group_local = tokens.shape[0] // CH
    local_width = w_query.shape[1]
    head_dev = local_width // HS
    seq_count = readers.shape[0] // group_local
    row_count = seq_count // ROW
    tp_count = w_out.shape[1] // local_width
    chip_count = tp_count // PAIR
    chip_width = PAIR * local_width
    row_at = lax.axis_index("sy")
    seq_index = row_at * ROW + lax.axis_index("sx")
    core_at = lax.axis_index("tc")
    tp_index = lax.axis_index("tz") * PAIR + core_at
    first_group = seq_index * group_local

    out_blocks = w_out.reshape(local_width, chip_count, chip_width)
    w_out_chip = jnp.zeros((tp_count, local_width, chip_width), w_out.dtype)
    for shift in range(tp_count):
        target = (tp_index + shift) % tp_count
        piece = lax.dynamic_index_in_dim(out_blocks, target // PAIR, 1, False)
        if shift:
            pairs = [(i, (i + shift) % tp_count) for i in range(tp_count)]
            piece = lax.ppermute(piece, TP, pairs)
        w_out_chip = lax.dynamic_update_index_in_dim(
            w_out_chip, piece, (tp_index - shift) % tp_count, 0
        )
    w_out_chip = w_out_chip.reshape(tp_count * local_width, chip_width)

    local_lengths = lax.dynamic_slice_in_dim(lengths, first_group, group_local, 0)
    reader_rows = lax.dynamic_slice_in_dim(readers, first_group, group_local, 0)
    offsets = jnp.arange(CH, dtype=jnp.int32)
    live_mask = (offsets[None, :] < local_lengths[:, None]).reshape(-1)[:, None]
    key_rows = jnp.where(
        live_mask, jnp.dot(tokens, w_key, preferred_element_type=jnp.float32), 0.0
    ).astype(jnp.bfloat16)
    value_rows = jnp.where(
        live_mask, jnp.dot(tokens, w_value, preferred_element_type=jnp.float32), 0.0
    ).astype(jnp.bfloat16)
    w_query, w_out_chip = lax.optimization_barrier((w_query, w_out_chip))
    query_rows = jnp.dot(tokens, w_query, preferred_element_type=jnp.float32).astype(jnp.bfloat16)
    query_blocks = query_rows.reshape(group_local, CH, head_dev, HS)
    key_blocks = key_rows.reshape(group_local, CH, head_dev, HS)
    value_blocks = value_rows.reshape(group_local, CH, head_dev, HS)

    states = jnp.einsum(
        "cshd,cshe->chde", key_blocks, value_blocks, preferred_element_type=jnp.float32
    ).astype(jnp.bfloat16)

    local_readers = lax.dynamic_slice_in_dim(reader_rows, first_group, group_local, 1)
    last_row = local_readers[group_local - 1].at[group_local - 1].set(1)
    tail = jnp.einsum(
        "c,chde->hde", last_row.astype(jnp.bfloat16), states, preferred_element_type=jnp.float32
    )
    row_tails = lax.all_gather(tail, "sx", axis=0, tiled=False)
    row_lasts = (row_at * ROW + jnp.arange(ROW)) * group_local + group_local - 1
    in_row = readers[row_lasts[ROW - 1], row_lasts].at[ROW - 1].set(1).astype(jnp.float32)
    row_sum = (in_row[:, None, None, None] * row_tails).sum(0)
    row_sums = lax.all_gather(row_sum, "sy", axis=0, tiled=False)
    row_ends = (jnp.arange(row_count) * ROW + ROW - 1) * group_local + group_local - 1
    from_rows = readers[first_group, row_ends].astype(jnp.float32)
    from_row = readers[first_group, row_lasts].astype(jnp.float32)
    entering = (from_row[:, None, None, None] * row_tails).sum(0) + (
        from_rows[:, None, None, None] * row_sums
    ).sum(0)
    enters = local_readers[:, 0].at[0].set(1).astype(jnp.float32)
    carried_in = enters[:, None, None, None] * entering[None]
    own = jnp.einsum(
        "ce,ehij->chij",
        local_readers.astype(jnp.bfloat16),
        states,
        preferred_element_type=jnp.float32,
    )
    prefix = (carried_in + own).astype(jnp.bfloat16)

    carried = jnp.einsum(
        "cthd,chde->cthe", query_blocks, prefix, preferred_element_type=jnp.float32
    )
    scores = jnp.einsum(
        "cthd,cshd->chts", query_blocks, key_blocks, preferred_element_type=jnp.float32
    )
    causal = offsets[:, None] >= offsets[None, :]
    weights = jnp.where(causal[None, None], scores, 0.0).astype(jnp.bfloat16)
    within = jnp.einsum(
        "chts,cshe->cthe", weights, value_blocks, preferred_element_type=jnp.float32
    )
    length_float = lengths.astype(jnp.float32)
    keys_read = local_lengths.astype(jnp.float32) + jnp.dot(
        reader_rows.astype(jnp.float32), length_float, precision=lax.Precision.HIGHEST
    )
    row_scale = lax.rsqrt(HS * keys_read)
    mixed = (carried + within) * row_scale[:, None, None, None]
    mixed = jnp.where(live_mask.reshape(group_local, CH, 1, 1), mixed, 0.0).astype(jnp.bfloat16)
    mixed = mixed.reshape(group_local * CH, local_width)

    half = group_local * CH // PAIR
    pair_mixed = lax.all_gather(mixed, "tc", axis=1, tiled=True)
    mine = lax.dynamic_slice_in_dim(pair_mixed, core_at * half, half, 0)
    full = lax.all_gather(mine, "tz", axis=1, tiled=True)
    part = jnp.dot(full, w_out_chip, preferred_element_type=jnp.float32).astype(jnp.bfloat16)
    kept = lax.dynamic_slice_in_dim(part, core_at * local_width, local_width, 1)
    given = lax.dynamic_slice_in_dim(part, (1 - core_at) * local_width, local_width, 1)
    got = lax.ppermute(given, "tc", [(0, 1), (1, 0)])
    result = jnp.zeros((group_local * CH, local_width), part.dtype)
    result = lax.dynamic_update_slice_in_dim(result, kept, core_at * half, 0)
    return lax.dynamic_update_slice_in_dim(result, got, (1 - core_at) * half, 0)


def solution(mesh):
    seq_count, tp_count = mesh.devices.shape
    split = jax.sharding.Mesh(
        mesh.devices.reshape(seq_count // ROW, ROW, tp_count // PAIR, PAIR), ("sy", "sx", "tz", "tc")
    )
    seq = ("sy", "sx")
    tp = ("tz", "tc")
    return jax.shard_map(
        local,
        mesh=split,
        in_specs=(
            P(seq, None),
            P(None, tp),
            P(None, tp),
            P(None, tp),
            P(tp, None),
            P(),
            P(),
        ),
        out_specs=P(seq, tp),
        check_vma=False,
    )
```

```python
import jax
import jax.numpy as jnp
from jax import lax
from jax.sharding import PartitionSpec as P

HS = 128
CH = 128
ROW = 4
PAIR = 2


SEQ = ("sy", "sx")
TP = ("tz", "tc")


def local(tokens, w_query, w_key, w_value, w_out, readers, lengths):
    group_local = tokens.shape[0] // CH
    local_width = w_query.shape[1]
    head_dev = local_width // HS
    seq_count = readers.shape[0] // group_local
    row_count = seq_count // ROW
    tp_count = w_out.shape[1] // local_width
    row_at = lax.axis_index("sy")
    seq_index = row_at * ROW + lax.axis_index("sx")
    core_at = lax.axis_index("tc")
    tp_index = lax.axis_index("tz") * PAIR + core_at
    first_group = seq_index * group_local

    out_blocks = w_out.reshape(local_width, tp_count, local_width)
    w_out_cols = jnp.zeros((tp_count, local_width, local_width), w_out.dtype)
    for shift in range(tp_count):
        piece = lax.dynamic_index_in_dim(out_blocks, (tp_index + shift) % tp_count, 1, False)
        if shift:
            pairs = [(i, (i + shift) % tp_count) for i in range(tp_count)]
            piece = lax.ppermute(piece, TP, pairs)
        w_out_cols = lax.dynamic_update_index_in_dim(
            w_out_cols, piece, (tp_index - shift) % tp_count, 0
        )
    w_out_cols = w_out_cols.reshape(tp_count * local_width, local_width)

    local_lengths = lax.dynamic_slice_in_dim(lengths, first_group, group_local, 0)
    reader_rows = lax.dynamic_slice_in_dim(readers, first_group, group_local, 0)
    offsets = jnp.arange(CH, dtype=jnp.int32)
    live_mask = (offsets[None, :] < local_lengths[:, None]).reshape(-1)[:, None]
    key_rows = jnp.where(
        live_mask, jnp.dot(tokens, w_key, preferred_element_type=jnp.float32), 0.0
    ).astype(jnp.bfloat16)
    value_rows = jnp.where(
        live_mask, jnp.dot(tokens, w_value, preferred_element_type=jnp.float32), 0.0
    ).astype(jnp.bfloat16)
    w_query, w_out_cols = lax.optimization_barrier((w_query, w_out_cols))
    query_rows = jnp.dot(tokens, w_query, preferred_element_type=jnp.float32).astype(jnp.bfloat16)
    query_blocks = query_rows.reshape(group_local, CH, head_dev, HS)
    key_blocks = key_rows.reshape(group_local, CH, head_dev, HS)
    value_blocks = value_rows.reshape(group_local, CH, head_dev, HS)

    states = jnp.einsum(
        "cshd,cshe->chde", key_blocks, value_blocks, preferred_element_type=jnp.float32
    ).astype(jnp.bfloat16)

    local_readers = lax.dynamic_slice_in_dim(reader_rows, first_group, group_local, 1)
    last_row = local_readers[group_local - 1].at[group_local - 1].set(1)
    tail = jnp.einsum(
        "c,chde->hde", last_row.astype(jnp.bfloat16), states, preferred_element_type=jnp.float32
    )
    row_tails = lax.all_gather(tail, "sx", axis=0, tiled=False)
    row_lasts = (row_at * ROW + jnp.arange(ROW)) * group_local + group_local - 1
    in_row = readers[row_lasts[ROW - 1], row_lasts].at[ROW - 1].set(1).astype(jnp.float32)
    row_sum = (in_row[:, None, None, None] * row_tails).sum(0)
    row_sums = lax.all_gather(row_sum, "sy", axis=0, tiled=False)
    row_ends = (jnp.arange(row_count) * ROW + ROW - 1) * group_local + group_local - 1
    from_rows = readers[first_group, row_ends].astype(jnp.float32)
    from_row = readers[first_group, row_lasts].astype(jnp.float32)
    entering = (from_row[:, None, None, None] * row_tails).sum(0) + (
        from_rows[:, None, None, None] * row_sums
    ).sum(0)
    enters = local_readers[:, 0].at[0].set(1).astype(jnp.float32)
    carried_in = enters[:, None, None, None] * entering[None]
    own = jnp.einsum(
        "ce,ehij->chij",
        local_readers.astype(jnp.bfloat16),
        states,
        preferred_element_type=jnp.float32,
    )
    prefix = (carried_in + own).astype(jnp.bfloat16)

    carried = jnp.einsum(
        "cthd,chde->cthe", query_blocks, prefix, preferred_element_type=jnp.float32
    )
    scores = jnp.einsum(
        "cthd,cshd->chts", query_blocks, key_blocks, preferred_element_type=jnp.float32
    )
    causal = offsets[:, None] >= offsets[None, :]
    weights = jnp.where(causal[None, None], scores, 0.0).astype(jnp.bfloat16)
    within = jnp.einsum(
        "chts,cshe->cthe", weights, value_blocks, preferred_element_type=jnp.float32
    )
    length_float = lengths.astype(jnp.float32)
    keys_read = local_lengths.astype(jnp.float32) + jnp.dot(
        reader_rows.astype(jnp.float32), length_float, precision=lax.Precision.HIGHEST
    )
    row_scale = lax.rsqrt(HS * keys_read)
    mixed = (carried + within) * row_scale[:, None, None, None]
    mixed = jnp.where(live_mask.reshape(group_local, CH, 1, 1), mixed, 0.0).astype(jnp.bfloat16)
    mixed = mixed.reshape(group_local * CH, local_width)

    mixed_all = lax.all_gather(mixed, TP, axis=1, tiled=True)
    return jnp.dot(mixed_all, w_out_cols, preferred_element_type=jnp.float32).astype(jnp.bfloat16)


def solution(mesh):
    seq_count, tp_count = mesh.devices.shape
    split = jax.sharding.Mesh(
        mesh.devices.reshape(seq_count // ROW, ROW, tp_count // PAIR, PAIR), ("sy", "sx", "tz", "tc")
    )
    seq = ("sy", "sx")
    tp = ("tz", "tc")
    return jax.shard_map(
        local,
        mesh=split,
        in_specs=(
            P(seq, None),
            P(None, tp),
            P(None, tp),
            P(None, tp),
            P(tp, None),
            P(),
            P(),
        ),
        out_specs=P(seq, tp),
        check_vma=False,
    )
```

```python
import jax
import jax.numpy as jnp
from jax import lax
from jax.sharding import PartitionSpec as P

HS = 128
CH = 128
ROW = 4
PAIR = 2


SEQ = ("sy", "sx")
TP = ("tz", "tc")


def local(tokens, w_query, w_key, w_value, w_out, readers, lengths):
    group_local = tokens.shape[0] // CH
    local_width = w_query.shape[1]
    head_dev = local_width // HS
    seq_count = readers.shape[0] // group_local
    row_count = seq_count // ROW
    tp_count = w_out.shape[1] // local_width
    row_at = lax.axis_index("sy")
    seq_index = row_at * ROW + lax.axis_index("sx")
    core_at = lax.axis_index("tc")
    tp_index = lax.axis_index("tz") * PAIR + core_at
    first_group = seq_index * group_local

    w_out_all = lax.all_gather(w_out, TP, axis=0, tiled=True)
    w_out_cols = lax.dynamic_slice_in_dim(w_out_all, tp_index * local_width, local_width, 1)

    local_lengths = lax.dynamic_slice_in_dim(lengths, first_group, group_local, 0)
    reader_rows = lax.dynamic_slice_in_dim(readers, first_group, group_local, 0)
    offsets = jnp.arange(CH, dtype=jnp.int32)
    live_mask = (offsets[None, :] < local_lengths[:, None]).reshape(-1)[:, None]
    key_rows = jnp.where(
        live_mask, jnp.dot(tokens, w_key, preferred_element_type=jnp.float32), 0.0
    ).astype(jnp.bfloat16)
    value_rows = jnp.where(
        live_mask, jnp.dot(tokens, w_value, preferred_element_type=jnp.float32), 0.0
    ).astype(jnp.bfloat16)
    query_rows = jnp.dot(tokens, w_query, preferred_element_type=jnp.float32).astype(jnp.bfloat16)
    query_blocks = query_rows.reshape(group_local, CH, head_dev, HS)
    key_blocks = key_rows.reshape(group_local, CH, head_dev, HS)
    value_blocks = value_rows.reshape(group_local, CH, head_dev, HS)

    states = jnp.einsum(
        "cshd,cshe->chde", key_blocks, value_blocks, preferred_element_type=jnp.float32
    ).astype(jnp.bfloat16)

    local_readers = lax.dynamic_slice_in_dim(reader_rows, first_group, group_local, 1)
    last_row = local_readers[group_local - 1].at[group_local - 1].set(1)
    tail = jnp.einsum(
        "c,chde->hde", last_row.astype(jnp.bfloat16), states, preferred_element_type=jnp.float32
    )
    row_tails = lax.all_gather(tail, "sx", axis=0, tiled=False)
    row_lasts = (row_at * ROW + jnp.arange(ROW)) * group_local + group_local - 1
    in_row = readers[row_lasts[ROW - 1], row_lasts].at[ROW - 1].set(1).astype(jnp.float32)
    row_sum = (in_row[:, None, None, None] * row_tails).sum(0)
    row_sums = lax.all_gather(row_sum, "sy", axis=0, tiled=False)
    row_ends = (jnp.arange(row_count) * ROW + ROW - 1) * group_local + group_local - 1
    from_rows = readers[first_group, row_ends].astype(jnp.float32)
    from_row = readers[first_group, row_lasts].astype(jnp.float32)
    entering = (from_row[:, None, None, None] * row_tails).sum(0) + (
        from_rows[:, None, None, None] * row_sums
    ).sum(0)
    enters = local_readers[:, 0].at[0].set(1).astype(jnp.float32)
    carried_in = enters[:, None, None, None] * entering[None]
    own = jnp.einsum(
        "ce,ehij->chij",
        local_readers.astype(jnp.bfloat16),
        states,
        preferred_element_type=jnp.float32,
    )
    prefix = (carried_in + own).astype(jnp.bfloat16)

    carried = jnp.einsum(
        "cthd,chde->cthe", query_blocks, prefix, preferred_element_type=jnp.float32
    )
    scores = jnp.einsum(
        "cthd,cshd->chts", query_blocks, key_blocks, preferred_element_type=jnp.float32
    )
    causal = offsets[:, None] >= offsets[None, :]
    weights = jnp.where(causal[None, None], scores, 0.0).astype(jnp.bfloat16)
    within = jnp.einsum(
        "chts,cshe->cthe", weights, value_blocks, preferred_element_type=jnp.float32
    )
    length_float = lengths.astype(jnp.float32)
    keys_read = local_lengths.astype(jnp.float32) + jnp.dot(
        reader_rows.astype(jnp.float32), length_float, precision=lax.Precision.HIGHEST
    )
    row_scale = lax.rsqrt(HS * keys_read)
    mixed = (carried + within) * row_scale[:, None, None, None]
    mixed = jnp.where(live_mask.reshape(group_local, CH, 1, 1), mixed, 0.0).astype(jnp.bfloat16)
    mixed = mixed.reshape(group_local * CH, local_width)

    mixed, w_out_cols = lax.optimization_barrier((mixed, w_out_cols))
    mixed_all = lax.all_gather(mixed, TP, axis=1, tiled=True)
    return jnp.dot(mixed_all, w_out_cols, preferred_element_type=jnp.float32).astype(jnp.bfloat16)


def solution(mesh):
    seq_count, tp_count = mesh.devices.shape
    split = jax.sharding.Mesh(
        mesh.devices.reshape(seq_count // ROW, ROW, tp_count // PAIR, PAIR), ("sy", "sx", "tz", "tc")
    )
    seq = ("sy", "sx")
    tp = ("tz", "tc")
    return jax.shard_map(
        local,
        mesh=split,
        in_specs=(
            P(seq, None),
            P(None, tp),
            P(None, tp),
            P(None, tp),
            P(tp, None),
            P(),
            P(),
        ),
        out_specs=P(seq, tp),
        check_vma=False,
    )
```

```python
import jax
import jax.numpy as jnp
from jax import lax
from jax.sharding import PartitionSpec as P

HS = 128
CH = 128
ROW = 4
PAIR = 2


SEQ = ("sy", "sx")
TP = ("tz", "tc")


def local(tokens, w_query, w_key, w_value, w_out, readers, lengths):
    group_local = tokens.shape[0] // CH
    local_width = w_query.shape[1]
    head_dev = local_width // HS
    seq_count = readers.shape[0] // group_local
    row_count = seq_count // ROW
    tp_count = w_out.shape[1] // local_width
    row_at = lax.axis_index("sy")
    seq_index = row_at * ROW + lax.axis_index("sx")
    core_at = lax.axis_index("tc")
    tp_index = lax.axis_index("tz") * PAIR + core_at
    first_group = seq_index * group_local

    w_out_all = lax.all_gather(w_out, TP, axis=0, tiled=True)

    local_lengths = lax.dynamic_slice_in_dim(lengths, first_group, group_local, 0)
    reader_rows = lax.dynamic_slice_in_dim(readers, first_group, group_local, 0)
    offsets = jnp.arange(CH, dtype=jnp.int32)
    live_mask = (offsets[None, :] < local_lengths[:, None]).reshape(-1)[:, None]
    key_rows = jnp.where(
        live_mask, jnp.dot(tokens, w_key, preferred_element_type=jnp.float32), 0.0
    ).astype(jnp.bfloat16)
    value_rows = jnp.where(
        live_mask, jnp.dot(tokens, w_value, preferred_element_type=jnp.float32), 0.0
    ).astype(jnp.bfloat16)
    query_rows = jnp.dot(tokens, w_query, preferred_element_type=jnp.float32).astype(jnp.bfloat16)
    query_blocks = query_rows.reshape(group_local, CH, head_dev, HS)
    key_blocks = key_rows.reshape(group_local, CH, head_dev, HS)
    value_blocks = value_rows.reshape(group_local, CH, head_dev, HS)

    states = jnp.einsum(
        "cshd,cshe->chde", key_blocks, value_blocks, preferred_element_type=jnp.float32
    ).astype(jnp.bfloat16)

    local_readers = lax.dynamic_slice_in_dim(reader_rows, first_group, group_local, 1)
    last_row = local_readers[group_local - 1].at[group_local - 1].set(1)
    tail = jnp.einsum(
        "c,chde->hde", last_row.astype(jnp.bfloat16), states, preferred_element_type=jnp.float32
    )
    row_tails = lax.all_gather(tail, "sx", axis=0, tiled=False)
    row_lasts = (row_at * ROW + jnp.arange(ROW)) * group_local + group_local - 1
    in_row = readers[row_lasts[ROW - 1], row_lasts].at[ROW - 1].set(1).astype(jnp.float32)
    row_sum = (in_row[:, None, None, None] * row_tails).sum(0)
    row_sums = lax.all_gather(row_sum, "sy", axis=0, tiled=False)
    row_ends = (jnp.arange(row_count) * ROW + ROW - 1) * group_local + group_local - 1
    from_rows = readers[first_group, row_ends].astype(jnp.float32)
    from_row = readers[first_group, row_lasts].astype(jnp.float32)
    entering = (from_row[:, None, None, None] * row_tails).sum(0) + (
        from_rows[:, None, None, None] * row_sums
    ).sum(0)
    enters = local_readers[:, 0].at[0].set(1).astype(jnp.float32)
    carried_in = enters[:, None, None, None] * entering[None]
    own = jnp.einsum(
        "ce,ehij->chij",
        local_readers.astype(jnp.bfloat16),
        states,
        preferred_element_type=jnp.float32,
    )
    prefix = (carried_in + own).astype(jnp.bfloat16)

    carried = jnp.einsum(
        "cthd,chde->cthe", query_blocks, prefix, preferred_element_type=jnp.float32
    )
    scores = jnp.einsum(
        "cthd,cshd->chts", query_blocks, key_blocks, preferred_element_type=jnp.float32
    )
    causal = offsets[:, None] >= offsets[None, :]
    weights = jnp.where(causal[None, None], scores, 0.0).astype(jnp.bfloat16)
    within = jnp.einsum(
        "chts,cshe->cthe", weights, value_blocks, preferred_element_type=jnp.float32
    )
    length_float = lengths.astype(jnp.float32)
    keys_read = local_lengths.astype(jnp.float32) + jnp.dot(
        reader_rows.astype(jnp.float32), length_float, precision=lax.Precision.HIGHEST
    )
    row_scale = lax.rsqrt(HS * keys_read)
    mixed = (carried + within) * row_scale[:, None, None, None]
    mixed = jnp.where(live_mask.reshape(group_local, CH, 1, 1), mixed, 0.0).astype(jnp.bfloat16)
    mixed = mixed.reshape(group_local * CH, local_width)

    mixed, w_out_all = lax.optimization_barrier((mixed, w_out_all))
    chip_at = lax.axis_index("tz")
    chip_count = tp_count // PAIR
    sources = [chip_at]
    blocks = [mixed]
    for step in (1, chip_count - 1, 2):
        pairs = [
            (z * PAIR + c, ((z + step) % chip_count) * PAIR + c)
            for z in range(chip_count)
            for c in range(PAIR)
        ]
        blocks.append(lax.ppermute(mixed, TP, pairs))
        sources.append((chip_at - step) % chip_count)
    same_core = jnp.concatenate(blocks, axis=1)
    other_core = lax.ppermute(same_core, "tc", [(0, 1), (1, 0)])
    column = tp_index * local_width

    def rows_of(chips, core):
        return jnp.concatenate(
            [
                lax.dynamic_slice(
                    w_out_all, ((z * PAIR + core) * local_width, column), (local_width, local_width)
                )
                for z in chips
            ],
            axis=0,
        )

    total = jnp.dot(same_core, rows_of(sources, core_at), preferred_element_type=jnp.float32)
    total = total + jnp.dot(
        other_core, rows_of(sources, 1 - core_at), preferred_element_type=jnp.float32
    )
    return total.astype(jnp.bfloat16)


def solution(mesh):
    seq_count, tp_count = mesh.devices.shape
    split = jax.sharding.Mesh(
        mesh.devices.reshape(seq_count // ROW, ROW, tp_count // PAIR, PAIR), ("sy", "sx", "tz", "tc")
    )
    seq = ("sy", "sx")
    tp = ("tz", "tc")
    return jax.shard_map(
        local,
        mesh=split,
        in_specs=(
            P(seq, None),
            P(None, tp),
            P(None, tp),
            P(None, tp),
            P(tp, None),
            P(),
            P(),
        ),
        out_specs=P(seq, tp),
        check_vma=False,
    )
```

```python
import jax
import jax.numpy as jnp
from jax import lax
from jax.sharding import PartitionSpec as P

HS = 128
CH = 128
ROW = 4
PAIR = 2


SEQ = ("sy", "sx")
TP = ("tz", "tc")


def local(tokens, w_query, w_key, w_value, w_out, readers, lengths):
    group_local = tokens.shape[0] // CH
    local_width = w_query.shape[1]
    head_dev = local_width // HS
    seq_count = readers.shape[0] // group_local
    row_count = seq_count // ROW
    tp_count = w_out.shape[1] // local_width
    row_at = lax.axis_index("sy")
    seq_index = row_at * ROW + lax.axis_index("sx")
    core_at = lax.axis_index("tc")
    tp_index = lax.axis_index("tz") * PAIR + core_at
    first_group = seq_index * group_local

    w_out_all = lax.all_gather(w_out, TP, axis=0, tiled=True)

    local_lengths = lax.dynamic_slice_in_dim(lengths, first_group, group_local, 0)
    reader_rows = lax.dynamic_slice_in_dim(readers, first_group, group_local, 0)
    offsets = jnp.arange(CH, dtype=jnp.int32)
    live_mask = (offsets[None, :] < local_lengths[:, None]).reshape(-1)[:, None]
    key_rows = jnp.where(
        live_mask, jnp.dot(tokens, w_key, preferred_element_type=jnp.float32), 0.0
    ).astype(jnp.bfloat16)
    value_rows = jnp.where(
        live_mask, jnp.dot(tokens, w_value, preferred_element_type=jnp.float32), 0.0
    ).astype(jnp.bfloat16)
    query_rows = jnp.dot(tokens, w_query, preferred_element_type=jnp.float32).astype(jnp.bfloat16)
    query_blocks = query_rows.reshape(group_local, CH, head_dev, HS)
    key_blocks = key_rows.reshape(group_local, CH, head_dev, HS)
    value_blocks = value_rows.reshape(group_local, CH, head_dev, HS)

    states = jnp.einsum(
        "cshd,cshe->chde", key_blocks, value_blocks, preferred_element_type=jnp.float32
    ).astype(jnp.bfloat16)

    local_readers = lax.dynamic_slice_in_dim(reader_rows, first_group, group_local, 1)
    last_row = local_readers[group_local - 1].at[group_local - 1].set(1)
    tail = jnp.einsum(
        "c,chde->hde", last_row.astype(jnp.bfloat16), states, preferred_element_type=jnp.float32
    )
    row_tails = lax.all_gather(tail, "sx", axis=0, tiled=False)
    row_end = (row_at * ROW + ROW - 1) * group_local + group_local - 1
    end_lasts = lax.dynamic_index_in_dim(readers, row_end, 0, False)
    end_lasts = end_lasts.reshape(seq_count, group_local)[:, group_local - 1]
    first_lasts = lax.dynamic_index_in_dim(readers, first_group, 0, False)
    first_lasts = first_lasts.reshape(seq_count, group_local)[:, group_local - 1].astype(jnp.float32)
    in_row = lax.dynamic_slice_in_dim(end_lasts, row_at * ROW, ROW).at[ROW - 1].set(1).astype(jnp.float32)
    row_sum = (in_row[:, None, None, None] * row_tails).sum(0)
    row_sums = lax.all_gather(row_sum, "sy", axis=0, tiled=False)
    from_rows = first_lasts.reshape(row_count, ROW)[:, ROW - 1]
    from_row = lax.dynamic_slice_in_dim(first_lasts, row_at * ROW, ROW)
    entering = (from_row[:, None, None, None] * row_tails).sum(0) + (
        from_rows[:, None, None, None] * row_sums
    ).sum(0)
    enters = local_readers[:, 0].at[0].set(1).astype(jnp.float32)
    carried_in = enters[:, None, None, None] * entering[None]
    own = jnp.einsum(
        "ce,ehij->chij",
        local_readers.astype(jnp.bfloat16),
        states,
        preferred_element_type=jnp.float32,
    )
    prefix = (carried_in + own).astype(jnp.bfloat16)

    carried = jnp.einsum(
        "cthd,chde->cthe", query_blocks, prefix, preferred_element_type=jnp.float32
    )
    scores = jnp.einsum(
        "cthd,cshd->chts", query_blocks, key_blocks, preferred_element_type=jnp.float32
    )
    causal = offsets[:, None] >= offsets[None, :]
    weights = jnp.where(causal[None, None], scores, 0.0).astype(jnp.bfloat16)
    within = jnp.einsum(
        "chts,cshe->cthe", weights, value_blocks, preferred_element_type=jnp.float32
    )
    length_float = lengths.astype(jnp.float32)
    keys_read = local_lengths.astype(jnp.float32) + jnp.dot(
        reader_rows.astype(jnp.float32), length_float, precision=lax.Precision.HIGHEST
    )
    row_scale = lax.rsqrt(HS * keys_read)
    mixed = (carried + within) * row_scale[:, None, None, None]
    mixed = jnp.where(live_mask.reshape(group_local, CH, 1, 1), mixed, 0.0).astype(jnp.bfloat16)
    mixed = mixed.reshape(group_local * CH, local_width)

    mixed, w_out_all = lax.optimization_barrier((mixed, w_out_all))
    chip_at = lax.axis_index("tz")
    chip_count = tp_count // PAIR
    column = tp_index * local_width

    def shifted(step):
        return [
            (z * PAIR + c, ((z + step) % chip_count) * PAIR + c)
            for z in range(chip_count)
            for c in range(PAIR)
        ]

    def rows_of(z, core):
        return lax.dynamic_slice(
            w_out_all, ((z * PAIR + core) * local_width, column), (local_width, local_width)
        )

    def term(block, z, core):
        return jnp.dot(block, rows_of(z, core), preferred_element_type=jnp.float32)

    from_below = lax.ppermute(mixed, TP, shifted(1))
    from_above = lax.ppermute(mixed, TP, shifted(chip_count - 1))
    below = (chip_at - 1) % chip_count
    above = (chip_at + 1) % chip_count
    across = (chip_at + 2) % chip_count
    first = jnp.concatenate([mixed, from_below, from_above], axis=1)
    sibling_first = lax.ppermute(first, "tc", [(0, 1), (1, 0)])
    forward = [
        (z * PAIR, ((z + 1) % chip_count) * PAIR) for z in range(chip_count)
    ] + [(z * PAIR + 1, ((z - 1) % chip_count) * PAIR + 1) for z in range(chip_count)]
    relayed = lax.ppermute(jnp.where(core_at == 0, from_below, from_above), TP, forward)
    sibling_relayed = lax.ppermute(relayed, "tc", [(0, 1), (1, 0)])
    other = 1 - core_at
    total = term(mixed, chip_at, core_at)
    total = total + term(from_below, below, core_at) + term(from_above, above, core_at)
    total = total + jnp.dot(
        sibling_first,
        jnp.concatenate(
            [rows_of(chip_at, other), rows_of(below, other), rows_of(above, other)], axis=0
        ),
        preferred_element_type=jnp.float32,
    )
    total = total + term(relayed, across, core_at) + term(sibling_relayed, across, other)
    return total.astype(jnp.bfloat16)


def solution(mesh):
    seq_count, tp_count = mesh.devices.shape
    split = jax.sharding.Mesh(
        mesh.devices.reshape(seq_count // ROW, ROW, tp_count // PAIR, PAIR), ("sy", "sx", "tz", "tc")
    )
    seq = ("sy", "sx")
    tp = ("tz", "tc")
    return jax.shard_map(
        local,
        mesh=split,
        in_specs=(
            P(seq, None),
            P(None, tp),
            P(None, tp),
            P(None, tp),
            P(tp, None),
            P(),
            P(),
        ),
        out_specs=P(seq, tp),
        check_vma=False,
    )
```

```python
import jax
import jax.numpy as jnp
from jax import lax
from jax.sharding import PartitionSpec as P

HS = 128
CH = 128
ROW = 4
PAIR = 2


SEQ = ("sy", "sx")
TP = ("tz", "tc")


def local(tokens, w_query, w_key, w_value, w_out, readers, lengths):
    group_local = tokens.shape[0] // CH
    local_width = w_query.shape[1]
    head_dev = local_width // HS
    seq_count = readers.shape[0] // group_local
    row_count = seq_count // ROW
    tp_count = w_out.shape[1] // local_width
    row_at = lax.axis_index("sy")
    seq_index = row_at * ROW + lax.axis_index("sx")
    core_at = lax.axis_index("tc")
    tp_index = lax.axis_index("tz") * PAIR + core_at
    first_group = seq_index * group_local

    w_out_all = lax.all_gather(w_out, TP, axis=0, tiled=True)

    local_lengths = lax.dynamic_slice_in_dim(lengths, first_group, group_local, 0)
    reader_rows = lax.dynamic_slice_in_dim(readers, first_group, group_local, 0)
    offsets = jnp.arange(CH, dtype=jnp.int32)
    live_mask = (offsets[None, :] < local_lengths[:, None]).reshape(-1)[:, None]
    key_rows = jnp.where(
        live_mask, jnp.dot(tokens, w_key, preferred_element_type=jnp.float32), 0.0
    ).astype(jnp.bfloat16)
    value_rows = jnp.where(
        live_mask, jnp.dot(tokens, w_value, preferred_element_type=jnp.float32), 0.0
    ).astype(jnp.bfloat16)
    query_rows = jnp.dot(tokens, w_query, preferred_element_type=jnp.float32).astype(jnp.bfloat16)
    query_blocks = query_rows.reshape(group_local, CH, head_dev, HS)
    key_blocks = key_rows.reshape(group_local, CH, head_dev, HS)
    value_blocks = value_rows.reshape(group_local, CH, head_dev, HS)

    states = jnp.einsum(
        "cshd,cshe->chde", key_blocks, value_blocks, preferred_element_type=jnp.float32
    ).astype(jnp.bfloat16)

    local_readers = lax.dynamic_slice_in_dim(reader_rows, first_group, group_local, 1)
    last_row = local_readers[group_local - 1].at[group_local - 1].set(1)
    tail = jnp.einsum(
        "c,chde->hde", last_row.astype(jnp.bfloat16), states, preferred_element_type=jnp.float32
    )
    col_at = lax.axis_index("sx")
    row_end = (row_at * ROW + ROW - 1) * group_local + group_local - 1
    end_lasts = lax.dynamic_index_in_dim(readers, row_end, 0, False)
    end_lasts = end_lasts.reshape(seq_count, group_local)[:, group_local - 1]
    first_lasts = lax.dynamic_index_in_dim(readers, first_group, 0, False)
    first_lasts = first_lasts.reshape(seq_count, group_local)[:, group_local - 1].astype(jnp.float32)
    in_row = lax.dynamic_slice_in_dim(end_lasts, row_at * ROW, ROW).at[ROW - 1].set(1).astype(jnp.float32)
    from_row = lax.dynamic_slice_in_dim(first_lasts, row_at * ROW, ROW)
    from_rows = first_lasts.reshape(row_count, ROW)[:, ROW - 1]
    row_sum = in_row[col_at] * tail
    entering = jnp.zeros_like(tail)
    for step in range(1, ROW):
        moved = lax.ppermute(tail, "sx", [(i, (i + step) % ROW) for i in range(ROW)])
        source = (col_at - step) % ROW
        row_sum = row_sum + in_row[source] * moved
        entering = entering + from_row[source] * moved
    for step in range(1, row_count):
        moved = lax.ppermute(row_sum, "sy", [(i, i + step) for i in range(row_count - step)])
        entering = entering + from_rows[jnp.maximum(row_at - step, 0)] * moved
    enters = local_readers[:, 0].at[0].set(1).astype(jnp.float32)
    carried_in = enters[:, None, None, None] * entering[None]
    own = jnp.einsum(
        "ce,ehij->chij",
        local_readers.astype(jnp.bfloat16),
        states,
        preferred_element_type=jnp.float32,
    )
    prefix = (carried_in + own).astype(jnp.bfloat16)

    carried = jnp.einsum(
        "cthd,chde->cthe", query_blocks, prefix, preferred_element_type=jnp.float32
    )
    scores = jnp.einsum(
        "cthd,cshd->chts", query_blocks, key_blocks, preferred_element_type=jnp.float32
    )
    causal = offsets[:, None] >= offsets[None, :]
    weights = jnp.where(causal[None, None], scores, 0.0).astype(jnp.bfloat16)
    within = jnp.einsum(
        "chts,cshe->cthe", weights, value_blocks, preferred_element_type=jnp.float32
    )
    length_float = lengths.astype(jnp.float32)
    keys_read = local_lengths.astype(jnp.float32) + jnp.dot(
        reader_rows.astype(jnp.float32), length_float, precision=lax.Precision.HIGHEST
    )
    row_scale = lax.rsqrt(HS * keys_read)
    mixed = (carried + within) * row_scale[:, None, None, None]
    mixed = jnp.where(live_mask.reshape(group_local, CH, 1, 1), mixed, 0.0).astype(jnp.bfloat16)
    mixed = mixed.reshape(group_local * CH, local_width)

    mixed, w_out_all = lax.optimization_barrier((mixed, w_out_all))
    chip_at = lax.axis_index("tz")
    chip_count = tp_count // PAIR
    column = tp_index * local_width

    def shifted(step):
        return [
            (z * PAIR + c, ((z + step) % chip_count) * PAIR + c)
            for z in range(chip_count)
            for c in range(PAIR)
        ]

    def rows_of(z, core):
        return lax.dynamic_slice(
            w_out_all, ((z * PAIR + core) * local_width, column), (local_width, local_width)
        )

    def term(block, z, core):
        return jnp.dot(block, rows_of(z, core), preferred_element_type=jnp.float32)

    from_below = lax.ppermute(mixed, TP, shifted(1))
    from_above = lax.ppermute(mixed, TP, shifted(chip_count - 1))
    below = (chip_at - 1) % chip_count
    above = (chip_at + 1) % chip_count
    across = (chip_at + 2) % chip_count
    first = jnp.concatenate([mixed, from_below, from_above], axis=1)
    sibling_first = lax.ppermute(first, "tc", [(0, 1), (1, 0)])
    forward = [
        (z * PAIR, ((z + 1) % chip_count) * PAIR) for z in range(chip_count)
    ] + [(z * PAIR + 1, ((z - 1) % chip_count) * PAIR + 1) for z in range(chip_count)]
    relayed = lax.ppermute(jnp.where(core_at == 0, from_below, from_above), TP, forward)
    sibling_relayed = lax.ppermute(relayed, "tc", [(0, 1), (1, 0)])
    other = 1 - core_at
    total = term(mixed, chip_at, core_at)
    total = total + term(from_below, below, core_at) + term(from_above, above, core_at)
    total = total + jnp.dot(
        sibling_first,
        jnp.concatenate(
            [rows_of(chip_at, other), rows_of(below, other), rows_of(above, other)], axis=0
        ),
        preferred_element_type=jnp.float32,
    )
    total = total + term(relayed, across, core_at) + term(sibling_relayed, across, other)
    return total.astype(jnp.bfloat16)


def solution(mesh):
    seq_count, tp_count = mesh.devices.shape
    split = jax.sharding.Mesh(
        mesh.devices.reshape(seq_count // ROW, ROW, tp_count // PAIR, PAIR), ("sy", "sx", "tz", "tc")
    )
    seq = ("sy", "sx")
    tp = ("tz", "tc")
    return jax.shard_map(
        local,
        mesh=split,
        in_specs=(
            P(seq, None),
            P(None, tp),
            P(None, tp),
            P(None, tp),
            P(tp, None),
            P(),
            P(),
        ),
        out_specs=P(seq, tp),
        check_vma=False,
    )
```

```python
import jax
import jax.numpy as jnp
from jax import lax
from jax.sharding import PartitionSpec as P

HS = 128
CH = 128
ROW = 4
PAIR = 2


SEQ = ("sy", "sx")
TP = ("tz", "tc")


def local(tokens, w_query, w_key, w_value, w_out, readers, lengths):
    group_local = tokens.shape[0] // CH
    local_width = w_query.shape[1]
    head_dev = local_width // HS
    seq_count = readers.shape[0] // group_local
    row_count = seq_count // ROW
    tp_count = w_out.shape[1] // local_width
    row_at = lax.axis_index("sy")
    seq_index = row_at * ROW + lax.axis_index("sx")
    core_at = lax.axis_index("tc")
    tp_index = lax.axis_index("tz") * PAIR + core_at
    first_group = seq_index * group_local

    w_out_all = lax.all_gather(w_out, TP, axis=0, tiled=True)

    local_lengths = lax.dynamic_slice_in_dim(lengths, first_group, group_local, 0)
    reader_rows = lax.dynamic_slice_in_dim(readers, first_group, group_local, 0)
    offsets = jnp.arange(CH, dtype=jnp.int32)
    live_mask = (offsets[None, :] < local_lengths[:, None]).reshape(-1)[:, None]
    key_rows = jnp.where(
        live_mask, jnp.dot(tokens, w_key, preferred_element_type=jnp.float32), 0.0
    ).astype(jnp.bfloat16)
    value_rows = jnp.where(
        live_mask, jnp.dot(tokens, w_value, preferred_element_type=jnp.float32), 0.0
    ).astype(jnp.bfloat16)
    query_rows = jnp.dot(tokens, w_query, preferred_element_type=jnp.float32).astype(jnp.bfloat16)
    query_blocks = query_rows.reshape(group_local, CH, head_dev, HS)
    key_blocks = key_rows.reshape(group_local, CH, head_dev, HS)
    value_blocks = value_rows.reshape(group_local, CH, head_dev, HS)

    states = jnp.einsum(
        "cshd,cshe->chde", key_blocks, value_blocks, preferred_element_type=jnp.float32
    ).astype(jnp.bfloat16)

    local_readers = lax.dynamic_slice_in_dim(reader_rows, first_group, group_local, 1)
    last_row = local_readers[group_local - 1].at[group_local - 1].set(1)
    tail = jnp.einsum(
        "c,chde->hde", last_row.astype(jnp.bfloat16), states, preferred_element_type=jnp.float32
    )
    row_tails = lax.all_gather(tail.astype(jnp.bfloat16), "sx", axis=0, tiled=False).astype(jnp.float32)
    row_end = (row_at * ROW + ROW - 1) * group_local + group_local - 1
    end_lasts = lax.dynamic_index_in_dim(readers, row_end, 0, False)
    end_lasts = end_lasts.reshape(seq_count, group_local)[:, group_local - 1]
    first_lasts = lax.dynamic_index_in_dim(readers, first_group, 0, False)
    first_lasts = first_lasts.reshape(seq_count, group_local)[:, group_local - 1].astype(jnp.float32)
    in_row = lax.dynamic_slice_in_dim(end_lasts, row_at * ROW, ROW).at[ROW - 1].set(1).astype(jnp.float32)
    row_sum = (in_row[:, None, None, None] * row_tails).sum(0)
    row_sums = lax.all_gather(row_sum.astype(jnp.bfloat16), "sy", axis=0, tiled=False).astype(jnp.float32)
    from_rows = first_lasts.reshape(row_count, ROW)[:, ROW - 1]
    from_row = lax.dynamic_slice_in_dim(first_lasts, row_at * ROW, ROW)
    entering = (from_row[:, None, None, None] * row_tails).sum(0) + (
        from_rows[:, None, None, None] * row_sums
    ).sum(0)
    enters = local_readers[:, 0].at[0].set(1).astype(jnp.float32)
    carried_in = enters[:, None, None, None] * entering[None]
    own = jnp.einsum(
        "ce,ehij->chij",
        local_readers.astype(jnp.bfloat16),
        states,
        preferred_element_type=jnp.float32,
    )
    prefix = (carried_in + own).astype(jnp.bfloat16)

    carried = jnp.einsum(
        "cthd,chde->cthe", query_blocks, prefix, preferred_element_type=jnp.float32
    )
    scores = jnp.einsum(
        "cthd,cshd->chts", query_blocks, key_blocks, preferred_element_type=jnp.float32
    )
    causal = offsets[:, None] >= offsets[None, :]
    weights = jnp.where(causal[None, None], scores, 0.0).astype(jnp.bfloat16)
    within = jnp.einsum(
        "chts,cshe->cthe", weights, value_blocks, preferred_element_type=jnp.float32
    )
    length_float = lengths.astype(jnp.float32)
    keys_read = local_lengths.astype(jnp.float32) + jnp.dot(
        reader_rows.astype(jnp.float32), length_float, precision=lax.Precision.HIGHEST
    )
    row_scale = lax.rsqrt(HS * keys_read)
    mixed = (carried + within) * row_scale[:, None, None, None]
    mixed = jnp.where(live_mask.reshape(group_local, CH, 1, 1), mixed, 0.0).astype(jnp.bfloat16)
    mixed = mixed.reshape(group_local * CH, local_width)

    mixed, w_out_all = lax.optimization_barrier((mixed, w_out_all))
    chip_at = lax.axis_index("tz")
    chip_count = tp_count // PAIR
    column = tp_index * local_width

    def shifted(step):
        return [
            (z * PAIR + c, ((z + step) % chip_count) * PAIR + c)
            for z in range(chip_count)
            for c in range(PAIR)
        ]

    def rows_of(z, core):
        return lax.dynamic_slice(
            w_out_all, ((z * PAIR + core) * local_width, column), (local_width, local_width)
        )

    def term(block, z, core):
        return jnp.dot(block, rows_of(z, core), preferred_element_type=jnp.float32)

    from_below = lax.ppermute(mixed, TP, shifted(1))
    from_above = lax.ppermute(mixed, TP, shifted(chip_count - 1))
    below = (chip_at - 1) % chip_count
    above = (chip_at + 1) % chip_count
    across = (chip_at + 2) % chip_count
    first = jnp.concatenate([mixed, from_below, from_above], axis=1)
    sibling_first = lax.ppermute(first, "tc", [(0, 1), (1, 0)])
    forward = [
        (z * PAIR, ((z + 1) % chip_count) * PAIR) for z in range(chip_count)
    ] + [(z * PAIR + 1, ((z - 1) % chip_count) * PAIR + 1) for z in range(chip_count)]
    relayed = lax.ppermute(jnp.where(core_at == 0, from_below, from_above), TP, forward)
    sibling_relayed = lax.ppermute(relayed, "tc", [(0, 1), (1, 0)])
    other = 1 - core_at
    total = term(mixed, chip_at, core_at)
    total = total + term(from_below, below, core_at) + term(from_above, above, core_at)
    total = total + jnp.dot(
        sibling_first,
        jnp.concatenate(
            [rows_of(chip_at, other), rows_of(below, other), rows_of(above, other)], axis=0
        ),
        preferred_element_type=jnp.float32,
    )
    total = total + term(relayed, across, core_at) + term(sibling_relayed, across, other)
    return total.astype(jnp.bfloat16)


def solution(mesh):
    seq_count, tp_count = mesh.devices.shape
    split = jax.sharding.Mesh(
        mesh.devices.reshape(seq_count // ROW, ROW, tp_count // PAIR, PAIR), ("sy", "sx", "tz", "tc")
    )
    seq = ("sy", "sx")
    tp = ("tz", "tc")
    return jax.shard_map(
        local,
        mesh=split,
        in_specs=(
            P(seq, None),
            P(None, tp),
            P(None, tp),
            P(None, tp),
            P(tp, None),
            P(),
            P(),
        ),
        out_specs=P(seq, tp),
        check_vma=False,
    )
```

```python
import jax
import jax.numpy as jnp
from jax import lax
from jax.sharding import PartitionSpec as P

HS = 128
CH = 128
ROW = 4
PAIR = 2


SEQ = ("sy", "sx")
TP = ("tz", "tc")


def local(tokens, w_query, w_key, w_value, w_out, readers, lengths):
    group_local = tokens.shape[0] // CH
    local_width = w_query.shape[1]
    head_dev = local_width // HS
    seq_count = readers.shape[0] // group_local
    row_count = seq_count // ROW
    tp_count = w_out.shape[1] // local_width
    row_at = lax.axis_index("sy")
    seq_index = row_at * ROW + lax.axis_index("sx")
    core_at = lax.axis_index("tc")
    tp_index = lax.axis_index("tz") * PAIR + core_at
    first_group = seq_index * group_local

    w_out_all = lax.all_gather(w_out, TP, axis=0, tiled=True)

    local_lengths = lax.dynamic_slice_in_dim(lengths, first_group, group_local, 0)
    reader_rows = lax.dynamic_slice_in_dim(readers, first_group, group_local, 0)
    offsets = jnp.arange(CH, dtype=jnp.int32)
    live_mask = (offsets[None, :] < local_lengths[:, None]).reshape(-1)[:, None]
    key_rows = jnp.where(
        live_mask, jnp.dot(tokens, w_key, preferred_element_type=jnp.float32), 0.0
    ).astype(jnp.bfloat16)
    value_rows = jnp.where(
        live_mask, jnp.dot(tokens, w_value, preferred_element_type=jnp.float32), 0.0
    ).astype(jnp.bfloat16)
    key_blocks = key_rows.reshape(group_local, CH, head_dev, HS)
    value_blocks = value_rows.reshape(group_local, CH, head_dev, HS)

    states = jnp.einsum(
        "cshd,cshe->chde", key_blocks, value_blocks, preferred_element_type=jnp.float32
    ).astype(jnp.bfloat16)

    local_readers = lax.dynamic_slice_in_dim(reader_rows, first_group, group_local, 1)
    last_row = local_readers[group_local - 1].at[group_local - 1].set(1)
    tail = jnp.einsum(
        "c,chde->hde", last_row.astype(jnp.bfloat16), states, preferred_element_type=jnp.float32
    )
    row_tails = lax.all_gather(tail, "sx", axis=0, tiled=False)
    row_end = (row_at * ROW + ROW - 1) * group_local + group_local - 1
    end_lasts = lax.dynamic_index_in_dim(readers, row_end, 0, False)
    end_lasts = end_lasts.reshape(seq_count, group_local)[:, group_local - 1]
    first_lasts = lax.dynamic_index_in_dim(readers, first_group, 0, False)
    first_lasts = first_lasts.reshape(seq_count, group_local)[:, group_local - 1].astype(jnp.float32)
    in_row = lax.dynamic_slice_in_dim(end_lasts, row_at * ROW, ROW).at[ROW - 1].set(1).astype(jnp.float32)
    row_sum = (in_row[:, None, None, None] * row_tails).sum(0)
    row_sums = lax.all_gather(row_sum, "sy", axis=0, tiled=False)
    from_rows = first_lasts.reshape(row_count, ROW)[:, ROW - 1]
    from_row = lax.dynamic_slice_in_dim(first_lasts, row_at * ROW, ROW)
    entering = (from_row[:, None, None, None] * row_tails).sum(0) + (
        from_rows[:, None, None, None] * row_sums
    ).sum(0)
    enters = local_readers[:, 0].at[0].set(1).astype(jnp.float32)
    carried_in = enters[:, None, None, None] * entering[None]
    own = jnp.einsum(
        "ce,ehij->chij",
        local_readers.astype(jnp.bfloat16),
        states,
        preferred_element_type=jnp.float32,
    )
    prefix = (carried_in + own).astype(jnp.bfloat16)

    length_float = lengths.astype(jnp.float32)
    keys_read = local_lengths.astype(jnp.float32) + jnp.dot(
        reader_rows.astype(jnp.float32), length_float, precision=lax.Precision.HIGHEST
    )
    row_scale = lax.rsqrt(HS * keys_read)
    causal = offsets[:, None] >= offsets[None, :]
    groups_live = live_mask.reshape(group_local, CH, 1, 1)

    def mix(lo, hi):
        query_rows = jnp.dot(
            tokens[lo * CH : hi * CH], w_query, preferred_element_type=jnp.float32
        ).astype(jnp.bfloat16)
        query_blocks = query_rows.reshape(hi - lo, CH, head_dev, HS)
        carried = jnp.einsum(
            "cthd,chde->cthe", query_blocks, prefix[lo:hi], preferred_element_type=jnp.float32
        )
        scores = jnp.einsum(
            "cthd,cshd->chts", query_blocks, key_blocks[lo:hi], preferred_element_type=jnp.float32
        )
        weights = jnp.where(causal[None, None], scores, 0.0).astype(jnp.bfloat16)
        within = jnp.einsum(
            "chts,cshe->cthe", weights, value_blocks[lo:hi], preferred_element_type=jnp.float32
        )
        mixed = (carried + within) * row_scale[lo:hi, None, None, None]
        mixed = jnp.where(groups_live[lo:hi], mixed, 0.0).astype(jnp.bfloat16)
        return mixed.reshape((hi - lo) * CH, local_width)

    chip_at = lax.axis_index("tz")
    chip_count = tp_count // PAIR
    column = tp_index * local_width
    below = (chip_at - 1) % chip_count
    above = (chip_at + 1) % chip_count
    across = (chip_at + 2) % chip_count
    other = 1 - core_at

    def shifted(step):
        return [
            (z * PAIR + c, ((z + step) % chip_count) * PAIR + c)
            for z in range(chip_count)
            for c in range(PAIR)
        ]

    forward = [
        (z * PAIR, ((z + 1) % chip_count) * PAIR) for z in range(chip_count)
    ] + [(z * PAIR + 1, ((z - 1) % chip_count) * PAIR + 1) for z in range(chip_count)]

    def project(mixed, w_all):
        def rows_of(z, core):
            return lax.dynamic_slice(
                w_all, ((z * PAIR + core) * local_width, column), (local_width, local_width)
            )

        def term(block, z, core):
            return jnp.dot(block, rows_of(z, core), preferred_element_type=jnp.float32)

        from_below = lax.ppermute(mixed, TP, shifted(1))
        from_above = lax.ppermute(mixed, TP, shifted(chip_count - 1))
        first = jnp.concatenate([mixed, from_below, from_above], axis=1)
        sibling_first = lax.ppermute(first, "tc", [(0, 1), (1, 0)])
        relayed = lax.ppermute(jnp.where(core_at == 0, from_below, from_above), TP, forward)
        sibling_relayed = lax.ppermute(relayed, "tc", [(0, 1), (1, 0)])
        total = term(mixed, chip_at, core_at)
        total = total + term(from_below, below, core_at) + term(from_above, above, core_at)
        total = total + jnp.dot(
            sibling_first,
            jnp.concatenate(
                [rows_of(chip_at, other), rows_of(below, other), rows_of(above, other)], axis=0
            ),
            preferred_element_type=jnp.float32,
        )
        total = total + term(relayed, across, core_at) + term(sibling_relayed, across, other)
        return total.astype(jnp.bfloat16)

    middle = group_local // 2
    early = mix(0, middle)
    early, w_out_all = lax.optimization_barrier((early, w_out_all))
    first_half = project(early, w_out_all)
    second_half = project(mix(middle, group_local), w_out_all)
    return jnp.concatenate([first_half, second_half], axis=0)


def solution(mesh):
    seq_count, tp_count = mesh.devices.shape
    split = jax.sharding.Mesh(
        mesh.devices.reshape(seq_count // ROW, ROW, tp_count // PAIR, PAIR), ("sy", "sx", "tz", "tc")
    )
    seq = ("sy", "sx")
    tp = ("tz", "tc")
    return jax.shard_map(
        local,
        mesh=split,
        in_specs=(
            P(seq, None),
            P(None, tp),
            P(None, tp),
            P(None, tp),
            P(tp, None),
            P(),
            P(),
        ),
        out_specs=P(seq, tp),
        check_vma=False,
    )
```

```python
import jax
import jax.numpy as jnp
from jax import lax
from jax.sharding import PartitionSpec as P

HS = 128
CH = 128
ROW = 4
PAIR = 2


SEQ = ("sy", "sx")
TP = ("tz", "tc")


def local(tokens, w_query, w_key, w_value, w_out, readers, lengths):
    group_local = tokens.shape[0] // CH
    local_width = w_query.shape[1]
    head_dev = local_width // HS
    seq_count = readers.shape[0] // group_local
    row_count = seq_count // ROW
    tp_count = w_out.shape[1] // local_width
    row_at = lax.axis_index("sy")
    seq_index = row_at * ROW + lax.axis_index("sx")
    core_at = lax.axis_index("tc")
    tp_index = lax.axis_index("tz") * PAIR + core_at
    first_group = seq_index * group_local

    w_out_all = lax.all_gather(w_out, TP, axis=0, tiled=True)

    local_lengths = lax.dynamic_slice_in_dim(lengths, first_group, group_local, 0)
    reader_rows = lax.dynamic_slice_in_dim(readers, first_group, group_local, 0)
    offsets = jnp.arange(CH, dtype=jnp.int32)
    live_mask = (offsets[None, :] < local_lengths[:, None]).reshape(-1)[:, None]
    key_rows = jnp.where(
        live_mask, jnp.dot(tokens, w_key, preferred_element_type=jnp.float32), 0.0
    ).astype(jnp.bfloat16)
    value_rows = jnp.where(
        live_mask, jnp.dot(tokens, w_value, preferred_element_type=jnp.float32), 0.0
    ).astype(jnp.bfloat16)
    query_rows = jnp.dot(tokens, w_query, preferred_element_type=jnp.float32).astype(jnp.bfloat16)
    query_groups = query_rows.reshape(group_local, CH, local_width)
    key_groups = key_rows.reshape(group_local, CH, local_width)
    value_groups = value_rows.reshape(group_local, CH, local_width)
    heads = [slice(h * HS, (h + 1) * HS) for h in range(head_dev)]
    states = jnp.stack(
        [
            jnp.einsum(
                "csd,cse->cde",
                key_groups[:, :, cut],
                value_groups[:, :, cut],
                preferred_element_type=jnp.float32,
            )
            for cut in heads
        ],
        axis=1,
    ).astype(jnp.bfloat16)

    local_readers = lax.dynamic_slice_in_dim(reader_rows, first_group, group_local, 1)
    last_row = local_readers[group_local - 1].at[group_local - 1].set(1)
    tail = jnp.einsum(
        "c,chde->hde", last_row.astype(jnp.bfloat16), states, preferred_element_type=jnp.float32
    )
    row_tails = lax.all_gather(tail, "sx", axis=0, tiled=False)
    row_end = (row_at * ROW + ROW - 1) * group_local + group_local - 1
    end_lasts = lax.dynamic_index_in_dim(readers, row_end, 0, False)
    end_lasts = end_lasts.reshape(seq_count, group_local)[:, group_local - 1]
    first_lasts = lax.dynamic_index_in_dim(readers, first_group, 0, False)
    first_lasts = first_lasts.reshape(seq_count, group_local)[:, group_local - 1].astype(jnp.float32)
    in_row = lax.dynamic_slice_in_dim(end_lasts, row_at * ROW, ROW).at[ROW - 1].set(1).astype(jnp.float32)
    row_sum = (in_row[:, None, None, None] * row_tails).sum(0)
    row_sums = lax.all_gather(row_sum, "sy", axis=0, tiled=False)
    from_rows = first_lasts.reshape(row_count, ROW)[:, ROW - 1]
    from_row = lax.dynamic_slice_in_dim(first_lasts, row_at * ROW, ROW)
    entering = (from_row[:, None, None, None] * row_tails).sum(0) + (
        from_rows[:, None, None, None] * row_sums
    ).sum(0)
    enters = local_readers[:, 0].at[0].set(1).astype(jnp.float32)
    carried_in = enters[:, None, None, None] * entering[None]
    own = jnp.einsum(
        "ce,ehij->chij",
        local_readers.astype(jnp.bfloat16),
        states,
        preferred_element_type=jnp.float32,
    )
    prefix = (carried_in + own).astype(jnp.bfloat16)

    length_float = lengths.astype(jnp.float32)
    keys_read = local_lengths.astype(jnp.float32) + jnp.dot(
        reader_rows.astype(jnp.float32), length_float, precision=lax.Precision.HIGHEST
    )
    row_scale = lax.rsqrt(HS * keys_read)
    causal = offsets[:, None] >= offsets[None, :]
    pieces = []
    for h, cut in enumerate(heads):
        query_h = query_groups[:, :, cut]
        carried = jnp.einsum(
            "ctd,cde->cte", query_h, prefix[:, h], preferred_element_type=jnp.float32
        )
        scores = jnp.einsum(
            "ctd,csd->cts", query_h, key_groups[:, :, cut], preferred_element_type=jnp.float32
        )
        weights = jnp.where(causal[None], scores, 0.0).astype(jnp.bfloat16)
        within = jnp.einsum(
            "cts,cse->cte", weights, value_groups[:, :, cut], preferred_element_type=jnp.float32
        )
        pieces.append((carried + within) * row_scale[:, None, None])
    mixed = jnp.concatenate(pieces, axis=2)
    mixed = jnp.where(live_mask.reshape(group_local, CH, 1), mixed, 0.0).astype(jnp.bfloat16)
    mixed = mixed.reshape(group_local * CH, local_width)

    mixed, w_out_all = lax.optimization_barrier((mixed, w_out_all))
    chip_at = lax.axis_index("tz")
    chip_count = tp_count // PAIR
    column = tp_index * local_width

    def shifted(step):
        return [
            (z * PAIR + c, ((z + step) % chip_count) * PAIR + c)
            for z in range(chip_count)
            for c in range(PAIR)
        ]

    def rows_of(z, core):
        return lax.dynamic_slice(
            w_out_all, ((z * PAIR + core) * local_width, column), (local_width, local_width)
        )

    def term(block, z, core):
        return jnp.dot(block, rows_of(z, core), preferred_element_type=jnp.float32)

    from_below = lax.ppermute(mixed, TP, shifted(1))
    from_above = lax.ppermute(mixed, TP, shifted(chip_count - 1))
    below = (chip_at - 1) % chip_count
    above = (chip_at + 1) % chip_count
    across = (chip_at + 2) % chip_count
    first = jnp.concatenate([mixed, from_below, from_above], axis=1)
    sibling_first = lax.ppermute(first, "tc", [(0, 1), (1, 0)])
    forward = [
        (z * PAIR, ((z + 1) % chip_count) * PAIR) for z in range(chip_count)
    ] + [(z * PAIR + 1, ((z - 1) % chip_count) * PAIR + 1) for z in range(chip_count)]
    relayed = lax.ppermute(jnp.where(core_at == 0, from_below, from_above), TP, forward)
    sibling_relayed = lax.ppermute(relayed, "tc", [(0, 1), (1, 0)])
    other = 1 - core_at
    total = term(mixed, chip_at, core_at)
    total = total + term(from_below, below, core_at) + term(from_above, above, core_at)
    total = total + jnp.dot(
        sibling_first,
        jnp.concatenate(
            [rows_of(chip_at, other), rows_of(below, other), rows_of(above, other)], axis=0
        ),
        preferred_element_type=jnp.float32,
    )
    total = total + term(relayed, across, core_at) + term(sibling_relayed, across, other)
    return total.astype(jnp.bfloat16)


def solution(mesh):
    seq_count, tp_count = mesh.devices.shape
    split = jax.sharding.Mesh(
        mesh.devices.reshape(seq_count // ROW, ROW, tp_count // PAIR, PAIR), ("sy", "sx", "tz", "tc")
    )
    seq = ("sy", "sx")
    tp = ("tz", "tc")
    return jax.shard_map(
        local,
        mesh=split,
        in_specs=(
            P(seq, None),
            P(None, tp),
            P(None, tp),
            P(None, tp),
            P(tp, None),
            P(),
            P(),
        ),
        out_specs=P(seq, tp),
        check_vma=False,
    )
```

```python
import jax
import jax.numpy as jnp
from jax import lax
from jax.sharding import PartitionSpec as P

HS = 128
CH = 128
ROW = 4
PAIR = 2


SEQ = ("sy", "sx")
TP = ("tz", "tc")


def local(tokens, w_query, w_key, w_value, w_out, readers, lengths):
    group_local = tokens.shape[0] // CH
    local_width = w_query.shape[1]
    head_dev = local_width // HS
    seq_count = readers.shape[0] // group_local
    row_count = seq_count // ROW
    tp_count = w_out.shape[1] // local_width
    row_at = lax.axis_index("sy")
    seq_index = row_at * ROW + lax.axis_index("sx")
    core_at = lax.axis_index("tc")
    tp_index = lax.axis_index("tz") * PAIR + core_at
    first_group = seq_index * group_local

    w_out_all = lax.all_gather(w_out, TP, axis=0, tiled=True)

    local_lengths = lax.dynamic_slice_in_dim(lengths, first_group, group_local, 0)
    reader_rows = lax.dynamic_slice_in_dim(readers, first_group, group_local, 0)
    offsets = jnp.arange(CH, dtype=jnp.int32)
    live_mask = (offsets[None, :] < local_lengths[:, None]).reshape(-1)[:, None]
    projected = jnp.dot(
        tokens,
        jnp.concatenate([w_key, w_value, w_query], axis=1),
        preferred_element_type=jnp.float32,
    )
    key_rows = jnp.where(live_mask, projected[:, :local_width], 0.0).astype(jnp.bfloat16)
    value_rows = jnp.where(
        live_mask, projected[:, local_width : 2 * local_width], 0.0
    ).astype(jnp.bfloat16)
    query_rows = projected[:, 2 * local_width :].astype(jnp.bfloat16)
    query_groups = query_rows.reshape(group_local, CH, local_width)
    key_groups = key_rows.reshape(group_local, CH, local_width)
    value_groups = value_rows.reshape(group_local, CH, local_width)
    heads = [slice(h * HS, (h + 1) * HS) for h in range(head_dev)]
    states = jnp.stack(
        [
            jnp.einsum(
                "csd,cse->cde",
                key_groups[:, :, cut],
                value_groups[:, :, cut],
                preferred_element_type=jnp.float32,
            )
            for cut in heads
        ],
        axis=1,
    ).astype(jnp.bfloat16)

    local_readers = lax.dynamic_slice_in_dim(reader_rows, first_group, group_local, 1)
    last_row = local_readers[group_local - 1].at[group_local - 1].set(1)
    tail = jnp.einsum(
        "c,chde->hde", last_row.astype(jnp.bfloat16), states, preferred_element_type=jnp.float32
    )
    row_tails = lax.all_gather(tail, "sx", axis=0, tiled=False)
    row_end = (row_at * ROW + ROW - 1) * group_local + group_local - 1
    end_lasts = lax.dynamic_index_in_dim(readers, row_end, 0, False)
    end_lasts = end_lasts.reshape(seq_count, group_local)[:, group_local - 1]
    first_lasts = lax.dynamic_index_in_dim(readers, first_group, 0, False)
    first_lasts = first_lasts.reshape(seq_count, group_local)[:, group_local - 1].astype(jnp.float32)
    in_row = lax.dynamic_slice_in_dim(end_lasts, row_at * ROW, ROW).at[ROW - 1].set(1).astype(jnp.float32)
    row_sum = (in_row[:, None, None, None] * row_tails).sum(0)
    row_sums = lax.all_gather(row_sum, "sy", axis=0, tiled=False)
    from_rows = first_lasts.reshape(row_count, ROW)[:, ROW - 1]
    from_row = lax.dynamic_slice_in_dim(first_lasts, row_at * ROW, ROW)
    entering = (from_row[:, None, None, None] * row_tails).sum(0) + (
        from_rows[:, None, None, None] * row_sums
    ).sum(0)
    enters = local_readers[:, 0].at[0].set(1).astype(jnp.float32)
    carried_in = enters[:, None, None, None] * entering[None]
    own = jnp.einsum(
        "ce,ehij->chij",
        local_readers.astype(jnp.bfloat16),
        states,
        preferred_element_type=jnp.float32,
    )
    prefix = (carried_in + own).astype(jnp.bfloat16)

    keys_read = (local_lengths + jnp.sum(reader_rows * lengths[None, :], axis=1)).astype(jnp.float32)
    row_scale = lax.rsqrt(HS * keys_read)
    causal = offsets[:, None] >= offsets[None, :]
    pieces = []
    for h, cut in enumerate(heads):
        query_h = query_groups[:, :, cut]
        carried = jnp.einsum(
            "ctd,cde->cte", query_h, prefix[:, h], preferred_element_type=jnp.float32
        )
        scores = jnp.einsum(
            "ctd,csd->cts", query_h, key_groups[:, :, cut], preferred_element_type=jnp.float32
        )
        weights = jnp.where(causal[None], scores, 0.0).astype(jnp.bfloat16)
        within = jnp.einsum(
            "cts,cse->cte", weights, value_groups[:, :, cut], preferred_element_type=jnp.float32
        )
        pieces.append((carried + within) * row_scale[:, None, None])
    mixed = jnp.concatenate(pieces, axis=2)
    mixed = jnp.where(live_mask.reshape(group_local, CH, 1), mixed, 0.0).astype(jnp.bfloat16)
    mixed = mixed.reshape(group_local * CH, local_width)

    mixed, w_out_all = lax.optimization_barrier((mixed, w_out_all))
    chip_at = lax.axis_index("tz")
    chip_count = tp_count // PAIR
    column = tp_index * local_width

    def shifted(step):
        return [
            (z * PAIR + c, ((z + step) % chip_count) * PAIR + c)
            for z in range(chip_count)
            for c in range(PAIR)
        ]

    def rows_of(z, core):
        return lax.dynamic_slice(
            w_out_all, ((z * PAIR + core) * local_width, column), (local_width, local_width)
        )

    def term(block, z, core):
        return jnp.dot(block, rows_of(z, core), preferred_element_type=jnp.float32)

    from_below = lax.ppermute(mixed, TP, shifted(1))
    from_above = lax.ppermute(mixed, TP, shifted(chip_count - 1))
    below = (chip_at - 1) % chip_count
    above = (chip_at + 1) % chip_count
    across = (chip_at + 2) % chip_count
    first = jnp.concatenate([mixed, from_below, from_above], axis=1)
    sibling_first = lax.ppermute(first, "tc", [(0, 1), (1, 0)])
    forward = [
        (z * PAIR, ((z + 1) % chip_count) * PAIR) for z in range(chip_count)
    ] + [(z * PAIR + 1, ((z - 1) % chip_count) * PAIR + 1) for z in range(chip_count)]
    relayed = lax.ppermute(jnp.where(core_at == 0, from_below, from_above), TP, forward)
    sibling_relayed = lax.ppermute(relayed, "tc", [(0, 1), (1, 0)])
    other = 1 - core_at
    total = term(mixed, chip_at, core_at)
    total = total + term(from_below, below, core_at) + term(from_above, above, core_at)
    total = total + jnp.dot(
        sibling_first,
        jnp.concatenate(
            [rows_of(chip_at, other), rows_of(below, other), rows_of(above, other)], axis=0
        ),
        preferred_element_type=jnp.float32,
    )
    total = total + term(relayed, across, core_at) + term(sibling_relayed, across, other)
    return total.astype(jnp.bfloat16)


def solution(mesh):
    seq_count, tp_count = mesh.devices.shape
    split = jax.sharding.Mesh(
        mesh.devices.reshape(seq_count // ROW, ROW, tp_count // PAIR, PAIR), ("sy", "sx", "tz", "tc")
    )
    seq = ("sy", "sx")
    tp = ("tz", "tc")
    return jax.shard_map(
        local,
        mesh=split,
        in_specs=(
            P(seq, None),
            P(None, tp),
            P(None, tp),
            P(None, tp),
            P(tp, None),
            P(),
            P(),
        ),
        out_specs=P(seq, tp),
        check_vma=False,
    )
```

```python
import jax
import jax.numpy as jnp
from jax import lax
from jax.sharding import PartitionSpec as P


HS = 128
CH = 128
ROW = 4
PAIR = 2


TP = ("tz", "tc")


def layer(tokens, w_query, w_key, w_value, w_out, readers, lengths):
    group_local = tokens.shape[0] // CH
    local_width = w_query.shape[1]
    head_dev = local_width // HS
    seq_count = readers.shape[0] // group_local
    row_count = seq_count // ROW
    tp_count = w_out.shape[1] // local_width
    row_at = lax.axis_index("sy")
    seq_index = row_at * ROW + lax.axis_index("sx")
    core_at = lax.axis_index("tc")
    tp_index = lax.axis_index("tz") * PAIR + core_at
    first_group = seq_index * group_local

    w_out_all = lax.all_gather(w_out, TP, axis=0, tiled=True)

    local_lengths = lax.dynamic_slice_in_dim(lengths, first_group, group_local, 0)
    reader_rows = lax.dynamic_slice_in_dim(readers, first_group, group_local, 0)
    offsets = jnp.arange(CH, dtype=jnp.int32)
    live_mask = (offsets[None, :] < local_lengths[:, None]).reshape(-1)[:, None]
    projected = jnp.dot(
        tokens,
        jnp.concatenate([w_key, w_value, w_query], axis=1),
        preferred_element_type=jnp.float32,
    )
    key_rows = jnp.where(live_mask, projected[:, :local_width], 0.0).astype(jnp.bfloat16)
    value_rows = jnp.where(
        live_mask, projected[:, local_width : 2 * local_width], 0.0
    ).astype(jnp.bfloat16)
    query_rows = projected[:, 2 * local_width :].astype(jnp.bfloat16)
    query_groups = query_rows.reshape(group_local, CH, local_width)
    key_groups = key_rows.reshape(group_local, CH, local_width)
    value_groups = value_rows.reshape(group_local, CH, local_width)
    heads = [slice(h * HS, (h + 1) * HS) for h in range(head_dev)]
    states = jnp.stack(
        [
            jnp.einsum(
                "csd,cse->cde",
                key_groups[:, :, cut],
                value_groups[:, :, cut],
                preferred_element_type=jnp.float32,
            )
            for cut in heads
        ],
        axis=1,
    ).astype(jnp.bfloat16)

    local_readers = lax.dynamic_slice_in_dim(reader_rows, first_group, group_local, 1)
    last_row = local_readers[group_local - 1].at[group_local - 1].set(1)
    tail = jnp.einsum(
        "c,chde->hde", last_row.astype(jnp.bfloat16), states, preferred_element_type=jnp.float32
    )
    row_tails = lax.all_gather(tail, "sx", axis=0, tiled=False)
    row_end = (row_at * ROW + ROW - 1) * group_local + group_local - 1
    end_lasts = lax.dynamic_index_in_dim(readers, row_end, 0, False)
    end_lasts = end_lasts.reshape(seq_count, group_local)[:, group_local - 1]
    first_lasts = lax.dynamic_index_in_dim(readers, first_group, 0, False)
    first_lasts = first_lasts.reshape(seq_count, group_local)[:, group_local - 1].astype(jnp.float32)
    in_row = lax.dynamic_slice_in_dim(end_lasts, row_at * ROW, ROW).at[ROW - 1].set(1).astype(jnp.float32)
    row_sum = (in_row[:, None, None, None] * row_tails).sum(0)
    row_sums = lax.all_gather(row_sum, "sy", axis=0, tiled=False)
    from_rows = first_lasts.reshape(row_count, ROW)[:, ROW - 1]
    from_row = lax.dynamic_slice_in_dim(first_lasts, row_at * ROW, ROW)
    entering = (from_row[:, None, None, None] * row_tails).sum(0) + (
        from_rows[:, None, None, None] * row_sums
    ).sum(0)
    enters = local_readers[:, 0].at[0].set(1).astype(jnp.float32)
    carried_in = enters[:, None, None, None] * entering[None]
    own = jnp.einsum(
        "ce,ehij->chij",
        local_readers.astype(jnp.bfloat16),
        states,
        preferred_element_type=jnp.float32,
    )
    prefix = (carried_in + own).astype(jnp.bfloat16)

    keys_read = (local_lengths + jnp.sum(reader_rows * lengths[None, :], axis=1)).astype(jnp.float32)
    row_scale = lax.rsqrt(HS * keys_read)
    causal = offsets[:, None] >= offsets[None, :]
    pieces = []
    for h, cut in enumerate(heads):
        query_h = query_groups[:, :, cut]
        carried = jnp.einsum(
            "ctd,cde->cte", query_h, prefix[:, h], preferred_element_type=jnp.float32
        )
        scores = jnp.einsum(
            "ctd,csd->cts", query_h, key_groups[:, :, cut], preferred_element_type=jnp.float32
        )
        weights = jnp.where(causal[None], scores, 0.0).astype(jnp.bfloat16)
        within = jnp.einsum(
            "cts,cse->cte", weights, value_groups[:, :, cut], preferred_element_type=jnp.float32
        )
        pieces.append((carried + within) * row_scale[:, None, None])
    mixed = jnp.concatenate(pieces, axis=2)
    mixed = jnp.where(live_mask.reshape(group_local, CH, 1), mixed, 0.0).astype(jnp.bfloat16)
    mixed = mixed.reshape(group_local * CH, local_width)

    chip_at = lax.axis_index("tz")
    chip_count = tp_count // PAIR
    column = tp_index * local_width

    def shifted(step):
        return [
            (z * PAIR + c, ((z + step) % chip_count) * PAIR + c)
            for z in range(chip_count)
            for c in range(PAIR)
        ]

    def rows_of(z, core):
        return lax.dynamic_slice(
            w_out_all, ((z * PAIR + core) * local_width, column), (local_width, local_width)
        )

    def term(block, z, core):
        return jnp.dot(block, rows_of(z, core), preferred_element_type=jnp.float32)

    from_below = lax.ppermute(mixed, TP, shifted(1))
    from_above = lax.ppermute(mixed, TP, shifted(chip_count - 1))
    from_below, from_above, w_out_all = lax.optimization_barrier((from_below, from_above, w_out_all))
    below = (chip_at - 1) % chip_count
    above = (chip_at + 1) % chip_count
    across = (chip_at + 2) % chip_count
    first = jnp.concatenate([mixed, from_below, from_above], axis=1)
    sibling_first = lax.ppermute(first, "tc", [(0, 1), (1, 0)])
    forward = [
        (z * PAIR, ((z + 1) % chip_count) * PAIR) for z in range(chip_count)
    ] + [(z * PAIR + 1, ((z - 1) % chip_count) * PAIR + 1) for z in range(chip_count)]
    relayed = lax.ppermute(jnp.where(core_at == 0, from_below, from_above), TP, forward)
    sibling_relayed = lax.ppermute(relayed, "tc", [(0, 1), (1, 0)])
    other = 1 - core_at
    total = term(mixed, chip_at, core_at)
    total = total + term(from_below, below, core_at) + term(from_above, above, core_at)
    total = total + jnp.dot(
        sibling_first,
        jnp.concatenate(
            [rows_of(chip_at, other), rows_of(below, other), rows_of(above, other)], axis=0
        ),
        preferred_element_type=jnp.float32,
    )
    total = total + term(relayed, across, core_at) + term(sibling_relayed, across, other)
    return total.astype(jnp.bfloat16)


def solution(mesh):
    seq_count, tp_count = mesh.devices.shape
    split = jax.sharding.Mesh(
        mesh.devices.reshape(seq_count // ROW, ROW, tp_count // PAIR, PAIR), ("sy", "sx", "tz", "tc")
    )
    seq = ("sy", "sx")
    tp = ("tz", "tc")
    return jax.shard_map(
        layer,
        mesh=split,
        in_specs=(
            P(seq, None),
            P(None, tp),
            P(None, tp),
            P(None, tp),
            P(tp, None),
            P(),
            P(),
        ),
        out_specs=P(seq, tp),
        check_vma=False,
    )
```

```python
import jax
import jax.numpy as jnp
from jax import lax
from jax.sharding import PartitionSpec as P


HS = 128
CH = 128
ROW = 4
PAIR = 2


TP = ("tz", "tc")


def layer(tokens, w_query, w_key, w_value, w_out, readers, lengths):
    group_local = tokens.shape[0] // CH
    local_width = w_query.shape[1]
    head_dev = local_width // HS
    seq_count = readers.shape[0] // group_local
    row_count = seq_count // ROW
    tp_count = w_out.shape[1] // local_width
    row_at = lax.axis_index("sy")
    seq_index = row_at * ROW + lax.axis_index("sx")
    core_at = lax.axis_index("tc")
    tp_index = lax.axis_index("tz") * PAIR + core_at
    first_group = seq_index * group_local

    w_out_all = lax.all_gather(w_out, TP, axis=0, tiled=True)

    local_lengths = lax.dynamic_slice_in_dim(lengths, first_group, group_local, 0)
    reader_rows = lax.dynamic_slice_in_dim(readers, first_group, group_local, 0)
    offsets = jnp.arange(CH, dtype=jnp.int32)
    live_mask = (offsets[None, :] < local_lengths[:, None]).reshape(-1)[:, None]
    projected = jnp.dot(
        tokens,
        jnp.concatenate([w_key, w_value, w_query], axis=1),
        preferred_element_type=jnp.float32,
    )
    key_rows = jnp.where(live_mask, projected[:, :local_width], 0.0).astype(jnp.bfloat16)
    value_rows = jnp.where(
        live_mask, projected[:, local_width : 2 * local_width], 0.0
    ).astype(jnp.bfloat16)
    query_rows = projected[:, 2 * local_width :].astype(jnp.bfloat16)
    query_groups = query_rows.reshape(group_local, CH, local_width)
    key_groups = key_rows.reshape(group_local, CH, local_width)
    value_groups = value_rows.reshape(group_local, CH, local_width)
    heads = [slice(h * HS, (h + 1) * HS) for h in range(head_dev)]
    states = jnp.stack(
        [
            jnp.einsum(
                "csd,cse->cde",
                key_groups[:, :, cut],
                value_groups[:, :, cut],
                preferred_element_type=jnp.float32,
            )
            for cut in heads
        ],
        axis=1,
    ).astype(jnp.bfloat16)

    local_readers = lax.dynamic_slice_in_dim(reader_rows, first_group, group_local, 1)
    last_row = local_readers[group_local - 1].at[group_local - 1].set(1)
    tail = jnp.einsum(
        "c,chde->hde", last_row.astype(jnp.bfloat16), states, preferred_element_type=jnp.float32
    )
    row_tails = lax.all_gather(tail, "sx", axis=0, tiled=False)
    row_end = (row_at * ROW + ROW - 1) * group_local + group_local - 1
    end_lasts = lax.dynamic_index_in_dim(readers, row_end, 0, False)
    end_lasts = end_lasts.reshape(seq_count, group_local)[:, group_local - 1]
    first_lasts = lax.dynamic_index_in_dim(readers, first_group, 0, False)
    first_lasts = first_lasts.reshape(seq_count, group_local)[:, group_local - 1].astype(jnp.float32)
    in_row = lax.dynamic_slice_in_dim(end_lasts, row_at * ROW, ROW).at[ROW - 1].set(1).astype(jnp.float32)
    row_sum = (in_row[:, None, None, None] * row_tails).sum(0)
    row_sums = lax.all_gather(row_sum, "sy", axis=0, tiled=False)
    from_rows = first_lasts.reshape(row_count, ROW)[:, ROW - 1]
    from_row = lax.dynamic_slice_in_dim(first_lasts, row_at * ROW, ROW)
    entering = (from_row[:, None, None, None] * row_tails).sum(0) + (
        from_rows[:, None, None, None] * row_sums
    ).sum(0)
    enters = local_readers[:, 0].at[0].set(1).astype(jnp.float32)
    carried_in = enters[:, None, None, None] * entering[None]
    own = jnp.einsum(
        "ce,ehij->chij",
        local_readers.astype(jnp.bfloat16),
        states,
        preferred_element_type=jnp.float32,
    )
    prefix = (carried_in + own).astype(jnp.bfloat16)

    keys_read = (local_lengths + jnp.sum(reader_rows * lengths[None, :], axis=1)).astype(jnp.float32)
    row_scale = lax.rsqrt(HS * keys_read)
    causal = offsets[:, None] >= offsets[None, :]
    pieces = []
    for h, cut in enumerate(heads):
        query_h = query_groups[:, :, cut]
        carried = jnp.einsum(
            "ctd,cde->cte", query_h, prefix[:, h], preferred_element_type=jnp.float32
        )
        scores = jnp.einsum(
            "ctd,csd->cts", query_h, key_groups[:, :, cut], preferred_element_type=jnp.float32
        )
        weights = jnp.where(causal[None], scores, 0.0).astype(jnp.bfloat16)
        within = jnp.einsum(
            "cts,cse->cte", weights, value_groups[:, :, cut], preferred_element_type=jnp.float32
        )
        pieces.append((carried + within) * row_scale[:, None, None])
    mixed = jnp.concatenate(pieces, axis=2)
    mixed = jnp.where(live_mask.reshape(group_local, CH, 1), mixed, 0.0).astype(jnp.bfloat16)
    mixed = mixed.reshape(group_local * CH, local_width)

    chip_at = lax.axis_index("tz")
    chip_count = tp_count // PAIR
    column = tp_index * local_width

    def shifted(step):
        return [
            (z * PAIR + c, ((z + step) % chip_count) * PAIR + c)
            for z in range(chip_count)
            for c in range(PAIR)
        ]

    def rows_of(z, core):
        return lax.dynamic_slice(
            w_out_all, ((z * PAIR + core) * local_width, column), (local_width, local_width)
        )

    def term(block, z, core):
        return jnp.dot(block, rows_of(z, core), preferred_element_type=jnp.float32)

    from_below = lax.ppermute(mixed, TP, shifted(1))
    from_above = lax.ppermute(mixed, TP, shifted(chip_count - 1))
    mate = lax.ppermute(mixed, "tc", [(0, 1), (1, 0)])
    from_below, from_above, w_out_all = lax.optimization_barrier((from_below, from_above, w_out_all))
    below = (chip_at - 1) % chip_count
    above = (chip_at + 1) % chip_count
    across = (chip_at + 2) % chip_count
    first = jnp.concatenate([from_below, from_above], axis=1)
    sibling_first = lax.ppermute(first, "tc", [(0, 1), (1, 0)])
    forward = [
        (z * PAIR, ((z + 1) % chip_count) * PAIR) for z in range(chip_count)
    ] + [(z * PAIR + 1, ((z - 1) % chip_count) * PAIR + 1) for z in range(chip_count)]
    relayed = lax.ppermute(jnp.where(core_at == 0, from_below, from_above), TP, forward)
    sibling_relayed = lax.ppermute(relayed, "tc", [(0, 1), (1, 0)])
    other = 1 - core_at
    total = term(mixed, chip_at, core_at)
    total = total + term(from_below, below, core_at) + term(from_above, above, core_at)
    total = total + term(mate, chip_at, other)
    total = total + jnp.dot(
        sibling_first,
        jnp.concatenate([rows_of(below, other), rows_of(above, other)], axis=0),
        preferred_element_type=jnp.float32,
    )
    total = total + term(relayed, across, core_at) + term(sibling_relayed, across, other)
    return total.astype(jnp.bfloat16)


def solution(mesh):
    seq_count, tp_count = mesh.devices.shape
    split = jax.sharding.Mesh(
        mesh.devices.reshape(seq_count // ROW, ROW, tp_count // PAIR, PAIR), ("sy", "sx", "tz", "tc")
    )
    seq = ("sy", "sx")
    tp = ("tz", "tc")
    return jax.shard_map(
        layer,
        mesh=split,
        in_specs=(
            P(seq, None),
            P(None, tp),
            P(None, tp),
            P(None, tp),
            P(tp, None),
            P(),
            P(),
        ),
        out_specs=P(seq, tp),
        check_vma=False,
    )
```

```python
import jax
import jax.numpy as jnp
from jax import lax
from jax.sharding import PartitionSpec as P


HS = 128
CH = 128
ROW = 4
PAIR = 2


TP = ("tz", "tc")


def layer(tokens, w_query, w_key, w_value, w_out, readers, lengths):
    group_local = tokens.shape[0] // CH
    local_width = w_query.shape[1]
    head_dev = local_width // HS
    seq_count = readers.shape[0] // group_local
    row_count = seq_count // ROW
    tp_count = w_out.shape[1] // local_width
    row_at = lax.axis_index("sy")
    seq_index = row_at * ROW + lax.axis_index("sx")
    core_at = lax.axis_index("tc")
    tp_index = lax.axis_index("tz") * PAIR + core_at
    first_group = seq_index * group_local

    w_out_all = lax.all_gather(w_out, TP, axis=0, tiled=True)

    local_lengths = lax.dynamic_slice_in_dim(lengths, first_group, group_local, 0)
    reader_rows = lax.dynamic_slice_in_dim(readers, first_group, group_local, 0)
    offsets = jnp.arange(CH, dtype=jnp.int32)
    live_mask = (offsets[None, :] < local_lengths[:, None]).reshape(-1)[:, None]
    projected = jnp.dot(
        tokens,
        jnp.concatenate([w_key, w_value, w_query], axis=1),
        preferred_element_type=jnp.float32,
    )
    key_rows = jnp.where(live_mask, projected[:, :local_width], 0.0).astype(jnp.bfloat16)
    value_rows = jnp.where(
        live_mask, projected[:, local_width : 2 * local_width], 0.0
    ).astype(jnp.bfloat16)
    query_rows = projected[:, 2 * local_width :].astype(jnp.bfloat16)
    query_groups = query_rows.reshape(group_local, CH, local_width)
    key_groups = key_rows.reshape(group_local, CH, local_width)
    value_groups = value_rows.reshape(group_local, CH, local_width)
    heads = [slice(h * HS, (h + 1) * HS) for h in range(head_dev)]
    states = jnp.stack(
        [
            jnp.einsum(
                "csd,cse->cde",
                key_groups[:, :, cut],
                value_groups[:, :, cut],
                preferred_element_type=jnp.float32,
            )
            for cut in heads
        ],
        axis=1,
    ).astype(jnp.bfloat16)

    local_readers = lax.dynamic_slice_in_dim(reader_rows, first_group, group_local, 1)
    last_row = local_readers[group_local - 1].at[group_local - 1].set(1)
    tail = jnp.einsum(
        "c,chde->hde", last_row.astype(jnp.bfloat16), states, preferred_element_type=jnp.float32
    )
    row_tails = lax.all_gather(tail, "sx", axis=0, tiled=False)
    row_end = (row_at * ROW + ROW - 1) * group_local + group_local - 1
    end_lasts = lax.dynamic_index_in_dim(readers, row_end, 0, False)
    end_lasts = end_lasts.reshape(seq_count, group_local)[:, group_local - 1]
    first_lasts = lax.dynamic_index_in_dim(readers, first_group, 0, False)
    first_lasts = first_lasts.reshape(seq_count, group_local)[:, group_local - 1].astype(jnp.float32)
    in_row = lax.dynamic_slice_in_dim(end_lasts, row_at * ROW, ROW).at[ROW - 1].set(1).astype(jnp.float32)
    row_sum = (in_row[:, None, None, None] * row_tails).sum(0)
    row_sums = lax.all_gather(row_sum, "sy", axis=0, tiled=False)
    from_rows = first_lasts.reshape(row_count, ROW)[:, ROW - 1]
    from_row = lax.dynamic_slice_in_dim(first_lasts, row_at * ROW, ROW)
    entering = (from_row[:, None, None, None] * row_tails).sum(0) + (
        from_rows[:, None, None, None] * row_sums
    ).sum(0)
    enters = local_readers[:, 0].at[0].set(1).astype(jnp.float32)
    carried_in = enters[:, None, None, None] * entering[None]
    own = jnp.einsum(
        "ce,ehij->chij",
        local_readers.astype(jnp.bfloat16),
        states,
        preferred_element_type=jnp.float32,
    )
    prefix = (carried_in + own).astype(jnp.bfloat16)

    keys_read = (local_lengths + jnp.sum(reader_rows * lengths[None, :], axis=1)).astype(jnp.float32)
    row_scale = lax.rsqrt(HS * keys_read)
    causal = offsets[:, None] >= offsets[None, :]
    pieces = []
    for h, cut in enumerate(heads):
        query_h = query_groups[:, :, cut]
        carried = jnp.einsum(
            "ctd,cde->cte", query_h, prefix[:, h], preferred_element_type=jnp.float32
        )
        scores = jnp.einsum(
            "ctd,csd->cts", query_h, key_groups[:, :, cut], preferred_element_type=jnp.float32
        )
        weights = jnp.where(causal[None], scores, 0.0).astype(jnp.bfloat16)
        within = jnp.einsum(
            "cts,cse->cte", weights, value_groups[:, :, cut], preferred_element_type=jnp.float32
        )
        pieces.append((carried + within) * row_scale[:, None, None])
    mixed = jnp.concatenate(pieces, axis=2)
    mixed = jnp.where(live_mask.reshape(group_local, CH, 1), mixed, 0.0).astype(jnp.bfloat16)
    mixed = mixed.reshape(group_local * CH, local_width)

    chip_at = lax.axis_index("tz")
    chip_count = tp_count // PAIR
    column = tp_index * local_width

    def shifted(step):
        return [
            (z * PAIR + c, ((z + step) % chip_count) * PAIR + c)
            for z in range(chip_count)
            for c in range(PAIR)
        ]

    def rows_of(z, core):
        return lax.dynamic_slice(
            w_out_all, ((z * PAIR + core) * local_width, column), (local_width, local_width)
        )

    def term(block, z, core):
        return jnp.dot(block, rows_of(z, core), preferred_element_type=jnp.float32)

    from_below = lax.ppermute(mixed, TP, shifted(1))
    from_above = lax.ppermute(mixed, TP, shifted(chip_count - 1))
    from_below, from_above, w_out_all = lax.optimization_barrier((from_below, from_above, w_out_all))
    below = (chip_at - 1) % chip_count
    above = (chip_at + 1) % chip_count
    across = (chip_at + 2) % chip_count
    first = jnp.concatenate([mixed, from_below, from_above], axis=1)
    sibling_first = lax.ppermute(first, "tc", [(0, 1), (1, 0)])
    up = [(z * PAIR, ((z + 1) % chip_count) * PAIR) for z in range(chip_count)]
    down = [(z * PAIR + 1, ((z - 1) % chip_count) * PAIR + 1) for z in range(chip_count)]
    relayed_up = lax.ppermute(from_below, TP, up)
    relayed_down = lax.ppermute(from_above, TP, down)
    sibling_up = lax.ppermute(relayed_up, "tc", [(0, 1)])
    sibling_down = lax.ppermute(relayed_down, "tc", [(1, 0)])
    other = 1 - core_at
    total = term(mixed, chip_at, core_at)
    total = total + term(from_below, below, core_at) + term(from_above, above, core_at)
    total = total + jnp.dot(
        sibling_first,
        jnp.concatenate(
            [rows_of(chip_at, other), rows_of(below, other), rows_of(above, other)], axis=0
        ),
        preferred_element_type=jnp.float32,
    )
    total = total + term(relayed_up, across, core_at) + term(relayed_down, across, core_at)
    total = total + term(sibling_up, across, other) + term(sibling_down, across, other)
    return total.astype(jnp.bfloat16)


def solution(mesh):
    seq_count, tp_count = mesh.devices.shape
    split = jax.sharding.Mesh(
        mesh.devices.reshape(seq_count // ROW, ROW, tp_count // PAIR, PAIR), ("sy", "sx", "tz", "tc")
    )
    seq = ("sy", "sx")
    tp = ("tz", "tc")
    return jax.shard_map(
        layer,
        mesh=split,
        in_specs=(
            P(seq, None),
            P(None, tp),
            P(None, tp),
            P(None, tp),
            P(tp, None),
            P(),
            P(),
        ),
        out_specs=P(seq, tp),
        check_vma=False,
    )
```

```python
import jax
import jax.numpy as jnp
from jax import lax
from jax.sharding import PartitionSpec as P


HS = 128
CH = 128
ROW = 4
PAIR = 2


TP = ("tz", "tc")


def layer(tokens, w_query, w_key, w_value, w_out, readers, lengths):
    group_local = tokens.shape[0] // CH
    local_width = w_query.shape[1]
    head_dev = local_width // HS
    seq_count = readers.shape[0] // group_local
    row_count = seq_count // ROW
    tp_count = w_out.shape[1] // local_width
    row_at = lax.axis_index("sy")
    seq_index = row_at * ROW + lax.axis_index("sx")
    core_at = lax.axis_index("tc")
    tp_index = lax.axis_index("tz") * PAIR + core_at
    first_group = seq_index * group_local


    local_lengths = lax.dynamic_slice_in_dim(lengths, first_group, group_local, 0)
    reader_rows = lax.dynamic_slice_in_dim(readers, first_group, group_local, 0)
    offsets = jnp.arange(CH, dtype=jnp.int32)
    live_mask = (offsets[None, :] < local_lengths[:, None]).reshape(-1)[:, None]
    projected = jnp.dot(
        tokens,
        jnp.concatenate([w_key, w_value, w_query], axis=1),
        preferred_element_type=jnp.float32,
    )
    key_rows = jnp.where(live_mask, projected[:, :local_width], 0.0).astype(jnp.bfloat16)
    value_rows = jnp.where(
        live_mask, projected[:, local_width : 2 * local_width], 0.0
    ).astype(jnp.bfloat16)
    query_rows = projected[:, 2 * local_width :].astype(jnp.bfloat16)
    query_groups = query_rows.reshape(group_local, CH, local_width)
    key_groups = key_rows.reshape(group_local, CH, local_width)
    value_groups = value_rows.reshape(group_local, CH, local_width)
    heads = [slice(h * HS, (h + 1) * HS) for h in range(head_dev)]
    states = jnp.stack(
        [
            jnp.einsum(
                "csd,cse->cde",
                key_groups[:, :, cut],
                value_groups[:, :, cut],
                preferred_element_type=jnp.float32,
            )
            for cut in heads
        ],
        axis=1,
    ).astype(jnp.bfloat16)

    local_readers = lax.dynamic_slice_in_dim(reader_rows, first_group, group_local, 1)
    last_row = local_readers[group_local - 1].at[group_local - 1].set(1)
    tail = jnp.einsum(
        "c,chde->hde", last_row.astype(jnp.bfloat16), states, preferred_element_type=jnp.float32
    )
    row_tails = lax.all_gather(tail, "sx", axis=0, tiled=False)
    row_end = (row_at * ROW + ROW - 1) * group_local + group_local - 1
    end_lasts = lax.dynamic_index_in_dim(readers, row_end, 0, False)
    end_lasts = end_lasts.reshape(seq_count, group_local)[:, group_local - 1]
    first_lasts = lax.dynamic_index_in_dim(readers, first_group, 0, False)
    first_lasts = first_lasts.reshape(seq_count, group_local)[:, group_local - 1].astype(jnp.float32)
    in_row = lax.dynamic_slice_in_dim(end_lasts, row_at * ROW, ROW).at[ROW - 1].set(1).astype(jnp.float32)
    row_sum = (in_row[:, None, None, None] * row_tails).sum(0)
    row_sums = lax.all_gather(row_sum, "sy", axis=0, tiled=False)
    from_rows = first_lasts.reshape(row_count, ROW)[:, ROW - 1]
    from_row = lax.dynamic_slice_in_dim(first_lasts, row_at * ROW, ROW)
    entering = (from_row[:, None, None, None] * row_tails).sum(0) + (
        from_rows[:, None, None, None] * row_sums
    ).sum(0)
    enters = local_readers[:, 0].at[0].set(1).astype(jnp.float32)
    carried_in = enters[:, None, None, None] * entering[None]
    own = jnp.einsum(
        "ce,ehij->chij",
        local_readers.astype(jnp.bfloat16),
        states,
        preferred_element_type=jnp.float32,
    )
    prefix = (carried_in + own).astype(jnp.bfloat16)

    keys_read = (local_lengths + jnp.sum(reader_rows * lengths[None, :], axis=1)).astype(jnp.float32)
    row_scale = lax.rsqrt(HS * keys_read)
    causal = offsets[:, None] >= offsets[None, :]
    pieces = []
    for h, cut in enumerate(heads):
        query_h = query_groups[:, :, cut]
        carried = jnp.einsum(
            "ctd,cde->cte", query_h, prefix[:, h], preferred_element_type=jnp.float32
        )
        scores = jnp.einsum(
            "ctd,csd->cts", query_h, key_groups[:, :, cut], preferred_element_type=jnp.float32
        )
        weights = jnp.where(causal[None], scores, 0.0).astype(jnp.bfloat16)
        within = jnp.einsum(
            "cts,cse->cte", weights, value_groups[:, :, cut], preferred_element_type=jnp.float32
        )
        pieces.append((carried + within) * row_scale[:, None, None])
    mixed = jnp.concatenate(pieces, axis=2)
    mixed = jnp.where(live_mask.reshape(group_local, CH, 1), mixed, 0.0).astype(jnp.bfloat16)
    mixed = mixed.reshape(group_local * CH, local_width)

    chip_at = lax.axis_index("tz")
    chip_count = tp_count // PAIR

    def shifted(step):
        return [
            (z * PAIR + c, ((z + step) % chip_count) * PAIR + c)
            for z in range(chip_count)
            for c in range(PAIR)
        ]

    def rows_of(z, core):
        return lax.dynamic_index_in_dim(w_out_cols, z * PAIR + core, 0, False)

    def term(block, z, core):
        return jnp.dot(block, rows_of(z, core), preferred_element_type=jnp.float32)

    from_below = lax.ppermute(mixed, TP, shifted(1))
    from_above = lax.ppermute(mixed, TP, shifted(chip_count - 1))
    mixed, w_out = lax.optimization_barrier((mixed, w_out))
    out_blocks = w_out.reshape(local_width, tp_count, local_width)
    w_out_cols = jnp.zeros((tp_count, local_width, local_width), w_out.dtype)
    for shift in range(tp_count):
        piece = lax.dynamic_index_in_dim(out_blocks, (tp_index + shift) % tp_count, 1, False)
        if shift:
            piece = lax.ppermute(piece, TP, [(i, (i + shift) % tp_count) for i in range(tp_count)])
        w_out_cols = lax.dynamic_update_index_in_dim(
            w_out_cols, piece, (tp_index - shift) % tp_count, 0
        )
    below = (chip_at - 1) % chip_count
    above = (chip_at + 1) % chip_count
    across = (chip_at + 2) % chip_count
    first = jnp.concatenate([mixed, from_below, from_above], axis=1)
    sibling_first = lax.ppermute(first, "tc", [(0, 1), (1, 0)])
    forward = [
        (z * PAIR, ((z + 1) % chip_count) * PAIR) for z in range(chip_count)
    ] + [(z * PAIR + 1, ((z - 1) % chip_count) * PAIR + 1) for z in range(chip_count)]
    relayed = lax.ppermute(jnp.where(core_at == 0, from_below, from_above), TP, forward)
    sibling_relayed = lax.ppermute(relayed, "tc", [(0, 1), (1, 0)])
    other = 1 - core_at
    total = term(mixed, chip_at, core_at)
    total = total + term(from_below, below, core_at) + term(from_above, above, core_at)
    total = total + jnp.dot(
        sibling_first,
        jnp.concatenate(
            [rows_of(chip_at, other), rows_of(below, other), rows_of(above, other)], axis=0
        ),
        preferred_element_type=jnp.float32,
    )
    total = total + term(relayed, across, core_at) + term(sibling_relayed, across, other)
    return total.astype(jnp.bfloat16)


def solution(mesh):
    seq_count, tp_count = mesh.devices.shape
    split = jax.sharding.Mesh(
        mesh.devices.reshape(seq_count // ROW, ROW, tp_count // PAIR, PAIR), ("sy", "sx", "tz", "tc")
    )
    seq = ("sy", "sx")
    tp = ("tz", "tc")
    return jax.shard_map(
        layer,
        mesh=split,
        in_specs=(
            P(seq, None),
            P(None, tp),
            P(None, tp),
            P(None, tp),
            P(tp, None),
            P(),
            P(),
        ),
        out_specs=P(seq, tp),
        check_vma=False,
    )
```

```python
import jax
import jax.numpy as jnp
from jax import lax
from jax.sharding import PartitionSpec as P


HS = 128
CH = 128
ROW = 4
PAIR = 2


TP = ("tz", "tc")


def layer(tokens, w_query, w_key, w_value, w_out, readers, lengths):
    group_local = tokens.shape[0] // CH
    local_width = w_query.shape[1]
    head_dev = local_width // HS
    seq_count = readers.shape[0] // group_local
    row_count = seq_count // ROW
    tp_count = w_out.shape[1] // local_width
    row_at = lax.axis_index("sy")
    seq_index = row_at * ROW + lax.axis_index("sx")
    core_at = lax.axis_index("tc")
    tp_index = lax.axis_index("tz") * PAIR + core_at
    first_group = seq_index * group_local


    local_lengths = lax.dynamic_slice_in_dim(lengths, first_group, group_local, 0)
    reader_rows = lax.dynamic_slice_in_dim(readers, first_group, group_local, 0)
    offsets = jnp.arange(CH, dtype=jnp.int32)
    live_mask = (offsets[None, :] < local_lengths[:, None]).reshape(-1)[:, None]
    projected = jnp.dot(
        tokens,
        jnp.concatenate([w_key, w_value, w_query], axis=1),
        preferred_element_type=jnp.float32,
    )
    key_rows = jnp.where(live_mask, projected[:, :local_width], 0.0).astype(jnp.bfloat16)
    value_rows = jnp.where(
        live_mask, projected[:, local_width : 2 * local_width], 0.0
    ).astype(jnp.bfloat16)
    query_rows = projected[:, 2 * local_width :].astype(jnp.bfloat16)
    query_groups = query_rows.reshape(group_local, CH, local_width)
    key_groups = key_rows.reshape(group_local, CH, local_width)
    value_groups = value_rows.reshape(group_local, CH, local_width)
    heads = [slice(h * HS, (h + 1) * HS) for h in range(head_dev)]
    states = jnp.stack(
        [
            jnp.einsum(
                "csd,cse->cde",
                key_groups[:, :, cut],
                value_groups[:, :, cut],
                preferred_element_type=jnp.float32,
            )
            for cut in heads
        ],
        axis=1,
    ).astype(jnp.bfloat16)

    local_readers = lax.dynamic_slice_in_dim(reader_rows, first_group, group_local, 1)
    last_row = local_readers[group_local - 1].at[group_local - 1].set(1)
    tail = jnp.einsum(
        "c,chde->hde", last_row.astype(jnp.bfloat16), states, preferred_element_type=jnp.float32
    )
    row_tails = lax.all_gather(tail, "sx", axis=0, tiled=False)
    row_end = (row_at * ROW + ROW - 1) * group_local + group_local - 1
    end_lasts = lax.dynamic_index_in_dim(readers, row_end, 0, False)
    end_lasts = end_lasts.reshape(seq_count, group_local)[:, group_local - 1]
    first_lasts = lax.dynamic_index_in_dim(readers, first_group, 0, False)
    first_lasts = first_lasts.reshape(seq_count, group_local)[:, group_local - 1].astype(jnp.float32)
    in_row = lax.dynamic_slice_in_dim(end_lasts, row_at * ROW, ROW).at[ROW - 1].set(1).astype(jnp.float32)
    row_sum = (in_row[:, None, None, None] * row_tails).sum(0)
    row_sums = lax.all_gather(row_sum, "sy", axis=0, tiled=False)
    from_rows = first_lasts.reshape(row_count, ROW)[:, ROW - 1]
    from_row = lax.dynamic_slice_in_dim(first_lasts, row_at * ROW, ROW)
    entering = (from_row[:, None, None, None] * row_tails).sum(0) + (
        from_rows[:, None, None, None] * row_sums
    ).sum(0)
    enters = local_readers[:, 0].at[0].set(1).astype(jnp.float32)
    carried_in = enters[:, None, None, None] * entering[None]
    own = jnp.einsum(
        "ce,ehij->chij",
        local_readers.astype(jnp.bfloat16),
        states,
        preferred_element_type=jnp.float32,
    )
    prefix = (carried_in + own).astype(jnp.bfloat16)

    keys_read = (local_lengths + jnp.sum(reader_rows * lengths[None, :], axis=1)).astype(jnp.float32)
    row_scale = lax.rsqrt(HS * keys_read)
    causal = offsets[:, None] >= offsets[None, :]
    pieces = []
    for h, cut in enumerate(heads):
        query_h = query_groups[:, :, cut]
        carried = jnp.einsum(
            "ctd,cde->cte", query_h, prefix[:, h], preferred_element_type=jnp.float32
        )
        scores = jnp.einsum(
            "ctd,csd->cts", query_h, key_groups[:, :, cut], preferred_element_type=jnp.float32
        )
        weights = jnp.where(causal[None], scores, 0.0).astype(jnp.bfloat16)
        within = jnp.einsum(
            "cts,cse->cte", weights, value_groups[:, :, cut], preferred_element_type=jnp.float32
        )
        pieces.append((carried + within) * row_scale[:, None, None])
    mixed = jnp.concatenate(pieces, axis=2)
    mixed = jnp.where(live_mask.reshape(group_local, CH, 1), mixed, 0.0).astype(jnp.bfloat16)
    mixed = mixed.reshape(group_local * CH, local_width)

    chip_at = lax.axis_index("tz")
    chip_count = tp_count // PAIR

    def shifted(step):
        return [
            (z * PAIR + c, ((z + step) % chip_count) * PAIR + c)
            for z in range(chip_count)
            for c in range(PAIR)
        ]

    def rows_of(z, core):
        return lax.dynamic_index_in_dim(w_out_cols, z * PAIR + core, 0, False)

    def term(block, z, core):
        return jnp.dot(block, rows_of(z, core), preferred_element_type=jnp.float32)

    from_below = lax.ppermute(mixed, TP, shifted(1))
    from_above = lax.ppermute(mixed, TP, shifted(chip_count - 1))
    out_blocks = jnp.transpose(w_out.reshape(local_width, tp_count, local_width), (1, 0, 2))
    mixed, out_blocks = lax.optimization_barrier((mixed, out_blocks))
    w_out_cols = jnp.zeros((tp_count, local_width, local_width), w_out.dtype)
    for shift in range(tp_count):
        piece = lax.dynamic_index_in_dim(out_blocks, (tp_index + shift) % tp_count, 0, False)
        if shift:
            piece = lax.ppermute(piece, TP, [(i, (i + shift) % tp_count) for i in range(tp_count)])
        w_out_cols = lax.dynamic_update_index_in_dim(
            w_out_cols, piece, (tp_index - shift) % tp_count, 0
        )
    below = (chip_at - 1) % chip_count
    above = (chip_at + 1) % chip_count
    across = (chip_at + 2) % chip_count
    first = jnp.concatenate([mixed, from_below, from_above], axis=1)
    sibling_first = lax.ppermute(first, "tc", [(0, 1), (1, 0)])
    forward = [
        (z * PAIR, ((z + 1) % chip_count) * PAIR) for z in range(chip_count)
    ] + [(z * PAIR + 1, ((z - 1) % chip_count) * PAIR + 1) for z in range(chip_count)]
    relayed = lax.ppermute(jnp.where(core_at == 0, from_below, from_above), TP, forward)
    sibling_relayed = lax.ppermute(relayed, "tc", [(0, 1), (1, 0)])
    other = 1 - core_at
    total = term(mixed, chip_at, core_at)
    total = total + term(from_below, below, core_at) + term(from_above, above, core_at)
    total = total + jnp.dot(
        sibling_first,
        jnp.concatenate(
            [rows_of(chip_at, other), rows_of(below, other), rows_of(above, other)], axis=0
        ),
        preferred_element_type=jnp.float32,
    )
    total = total + term(relayed, across, core_at) + term(sibling_relayed, across, other)
    return total.astype(jnp.bfloat16)


def solution(mesh):
    seq_count, tp_count = mesh.devices.shape
    split = jax.sharding.Mesh(
        mesh.devices.reshape(seq_count // ROW, ROW, tp_count // PAIR, PAIR), ("sy", "sx", "tz", "tc")
    )
    seq = ("sy", "sx")
    tp = ("tz", "tc")
    return jax.shard_map(
        layer,
        mesh=split,
        in_specs=(
            P(seq, None),
            P(None, tp),
            P(None, tp),
            P(None, tp),
            P(tp, None),
            P(),
            P(),
        ),
        out_specs=P(seq, tp),
        check_vma=False,
    )
```
